256 devices in a mesh: group: 32 (over z, y), tensor: 8 (over x, core).
Axes of the slice: x: 4, y: 4, z: 8, core: 2. Of those that a mesh axis runs over, the one named last changes fastest.
Arguments:
- query: bfloat16 [2, 1024, 2048], P(None, 'group', 'tensor'), may hold values from -80 to 80
- self_kv: bfloat16 [2, 1024, 2, 2048], P(None, 'group', None, 'tensor'), may hold values from -6 to 6
- kv_pages: bfloat16 [2, 1536, 16, 2, 2048], P(None, 'group', None, None, 'tensor'), may hold values from -6 to 6
- page_dest: int32 [1536, 1], replicated, may hold values from 0 to 31; in each aligned block of 48 rows (0 to 47, 48 to 95, ...) at most 3 rows name the same one
- page_request: int32 [1536], replicated, may hold values from 0 to 1
- score_len: int32 [64], P('group'), may hold values from 1 to 16
- out_proj: bfloat16 [2, 2048, 2048], P(None, 'tensor'), may hold values from -0.125 to 0.125
- residual: bfloat16 [2, 1024, 2048], P(None, ('group', 'tensor')), may hold values from -6 to 6
- norm_gain: float32 [2, 2048], replicated, may hold values from 0.5 to 40
- norm_bias: float32 [2, 2048], replicated, may hold values from -3 to 3
- vocab: bfloat16 [2, 2048, 196608], P(None, None, ('group', 'tensor')), may hold values from -0.3984375 to 0.3984375
- targets: int32 [1024], replicated, may hold values from 0 to 196607
Outputs:
- logprob: float32 [2, 1024], P(None, ('group', 'tensor'))
The draws below stay inside these ranges and needn't reach their ends.
Inputs may be any that keep to these rules, and one draw needn't show every extreme that they name: `page_dest`: the 48 pages of each aligned block (pages held by one group) go to any one group at most 3 times; some block sends exactly 3 to some group.
All inputs are finite; a program needn't handle non-finite values.
Results may differ from the reference program's by a relative error of at most 0.00097.
Values may be sent and summed in bfloat16 or wider, within the bound.
No kernel may reach another device: no remote copies, remote signals or barrier semaphores. Data moves between devices by JAX's collectives and lax.ppermute only.
A program may use at most 128 MiB of HBM per device.

```python
import math
import jax
import jax.numpy as jnp
import numpy as np
from jax import lax

D = 2048
HEADS = 16
HEAD_DIM = 128
REQ_GRP = 2
SCORE_LEN = 16
PAGE = 16
PAGES_DEV = 48
TOK_GRP = 32
TOKENS = 1024
REQUESTS = 64
PAGES = 1536
CAP = 3
VOCAB = 196608
N_GROUP = 32


def draw_query(key, part):
    first = jax.random.fold_in(key, 0)
    query_shape = (2, TOKENS, HEADS * HEAD_DIM)
    return jnp.clip(jax.random.normal(first, query_shape, jnp.float32), -6.0, 6.0).astype(jnp.bfloat16)


def draw_norm_gain(key, part):
    low_log = math.log(0.5)
    high_log = math.log(2.0)
    return jnp.exp(jax.random.uniform(key, (2, D), jnp.float32, low_log, high_log))


def touch_ends(values, key, smallest, high):
    place = [jax.random.randint(jax.random.fold_in(key, axis), (), 0, length) for axis, length in enumerate(values.shape)]
    longest = values.shape.index(max(values.shape))
    next_to = place[:longest] + [(place[longest] + 1) % values.shape[longest]] + place[longest + 1:]
    return values.at[tuple(place)].set(smallest).at[tuple(next_to)].set(high)


def block_scale(rng, extent, shards, least, high):
    def one(axis_at, blocks):
        steps = jax.random.uniform(jax.random.fold_in(jax.random.fold_in(rng, 6), axis_at), (blocks,), jnp.float32, least / len(shards), high / len(shards))
        return jnp.repeat(jnp.exp(steps), extent[axis_at] // blocks).reshape((-1,) + (1,) * (len(extent) - axis_at - 1))

    gain = one(*shards[0])
    for cut in shards[1:]:
        gain = gain * one(*cut)
    return gain


def wide_ids(own_key, extent, amount, skew):
    weights = [min(1 << octave, amount + 1 - (1 << octave)) * (1 << 20) // math.isqrt((1 << octave) ** skew) + 1 for octave in range((amount + 1).bit_length()) if 1 << octave <= amount]
    deviation = 1 + sum(weights) // (1 << 30)
    grid = np.cumsum(np.array([max(1, weight // deviation) for weight in weights]))
    lot = jax.random.randint(jax.random.fold_in(own_key, 1), extent, 0, int(grid[len(weights) - 1]))
    start = jnp.left_shift(1, jnp.searchsorted(jnp.asarray(grid, jnp.int32), lot, side="right").astype(jnp.int32))
    grade = start - 1 + jax.random.randint(jax.random.fold_in(own_key, 4), extent, 0, 1 << 30) % jnp.minimum(start, amount + 1 - start)
    return jax.random.permutation(jax.random.fold_in(own_key, 2), amount)[grade].astype(jnp.int32)


def deal_out(stream_key, own, number, rows, number_of, top, bound, lean):
    order = jax.random.permutation(stream_key, number_of)
    heavy_load, ordinary = portions_of(number_of, rows * top, bound, lean, True), portions_of(number_of, rows * top, bound, lean, False)
    places = jnp.arange(number_of)

    def named(sizes, offset_by):
        used = int((sizes > 0).sum())
        fixed = max(1, used // 4)
        shifted = fixed + (places - fixed + offset_by * (used - fixed)) % max(1, number_of - fixed)
        return jnp.zeros((number_of,), jnp.int32).at[order[jnp.where(places < fixed, places, shifted)]].set(jnp.asarray(sizes, jnp.int32))

    sizes = jnp.where(number % 4 == 0, named(heavy_load, number // 4), named(ordinary, number - number // 4 - 1))
    mixed = jax.random.permutation(jax.random.fold_in(own, 3), number_of)
    donor, sink = mixed[0:number_of // 2 * 2:2], mixed[1:number_of // 2 * 2:2]
    slack = jnp.minimum(sizes[donor] - 1, bound - sizes[sink]) // 2
    slack = jnp.where((donor == order[0]) | (sink == order[0]) | (sizes[sink] == 0), 0, jnp.maximum(slack, 0))
    shifted = jax.random.randint(jax.random.fold_in(own, 4), (number_of // 2,), 0, 1 << 20) % (slack + 1)
    sizes = sizes.at[donor].add(-shifted).at[sink].add(shifted)
    members = jnp.searchsorted(jnp.cumsum(sizes), jnp.arange(rows * top), side="right").astype(jnp.int32)
    table = members.reshape(top, rows).T
    table = table[jax.random.permutation(jax.random.fold_in(own, 1), rows)]
    offset_by = jax.random.randint(jax.random.fold_in(own, 2), (rows, 1), 0, top)
    return jnp.take_along_axis(table, (jnp.arange(top)[None, :] + offset_by) % top, axis=1)


def portions_of(amount, total, reach, lean, full):
    weights = [(1 << 20) // math.isqrt(rank ** lean) + 1 for rank in range(1, amount + 1)]
    largest = reach if full else min(reach, max(-(-total // amount), total * weights[0] // sum(weights)))
    least = 1 if total - largest >= amount - 1 else 0
    given, rest = [largest] + [least] * (amount - 1), total - largest - least * (amount - 1)
    while rest > 0:
        free = [i for i in range(1, amount) if given[i] < largest] or [i for i in range(1, amount) if given[i] < reach]
        pool, remaining = sum([weights[i] for i in free]), rest
        for i in free:
            extra = min(reach - given[i], max(1, remaining * weights[i] // pool), rest)
            given[i] = given[i] + extra
            rest = rest - extra
    return np.array(given)


def normal_values(key, dims, deviation, limit, cuts=(), kind=jnp.bfloat16):
    gain = block_scale(key, dims, cuts, -0.22, 0.18) if cuts else 1.0
    array = jax.random.normal(key, dims, jnp.float32) * deviation * gain
    return jnp.minimum(jnp.maximum(array, -limit), limit).astype(kind)


def setup_inputs(seed: int = 0) -> dict:
    seeds = jax.random.split(jax.random.key(seed), 13)
    query = draw_query(jax.random.fold_in(seeds[12], 71), 0)
    self_kv = normal_values(seeds[1], (2, TOKENS, 2, HEADS * HEAD_DIM), 1.0, 6.0, ((1, 32), (3, 8)))
    kv_pages = normal_values(seeds[2], (2, PAGES, PAGE, 2, HEADS * HEAD_DIM), 1.0, 6.0, ((1, 32), (4, 8)))
    page_dest_keys = jax.random.split(jax.random.fold_in(seeds[3], 1), PAGES // PAGES_DEV)
    page_dest_turns = jax.random.permutation(jax.random.fold_in(seeds[3], 3), PAGES // PAGES_DEV)
    page_dest = jax.vmap(lambda own, number: deal_out(jax.random.fold_in(seeds[3], 2), own, number, PAGES_DEV, N_GROUP, 1, CAP, 2))(page_dest_keys, page_dest_turns).reshape((PAGES, 1))
    page_request = touch_ends(jax.random.randint(seeds[4], (PAGES,), 0, REQ_GRP), jax.random.fold_in(seeds[4], 1), 0, REQ_GRP - 1).astype(jnp.int32)
    score_len = touch_ends(jax.random.randint(seeds[5], (REQUESTS,), 1, SCORE_LEN + 1), jax.random.fold_in(seeds[5], 1), 1, SCORE_LEN).astype(jnp.int32)
    out_proj = normal_values(seeds[6], (2, HEADS * HEAD_DIM, D), (HEADS * HEAD_DIM) ** -0.5, 0.125, ((1, 8),))
    residual = normal_values(seeds[7], (2, TOKENS, D), 1.0, 6.0, ((1, 256),))
    norm_gain = draw_norm_gain(jax.random.fold_in(seeds[12], 71), 0)
    norm_bias = normal_values(seeds[9], (2, D), 0.5, 3.0, (), jnp.float32)
    vocab = normal_values(seeds[10], (2, D, VOCAB), 0.066, 0.3984375, ((2, 256),))
    targets = touch_ends(wide_ids(seeds[11], (TOKENS,), VOCAB, 2), jax.random.fold_in(seeds[11], 3), 0, VOCAB - 1).astype(jnp.int32)
    return dict(query=query, self_kv=self_kv, kv_pages=kv_pages, page_dest=page_dest, page_request=page_request, score_len=score_len, out_proj=out_proj, residual=residual, norm_gain=norm_gain, norm_bias=norm_bias, vocab=vocab, targets=targets)


NEGATIVE = -1e+30
EPSILON = 1e-05

def route_tables(destination, request, groups, per_owner, capacity, requests):
    page_count = destination.shape[0]
    owner_group = jnp.arange(page_count, dtype=jnp.int32) // per_owner
    columns = jnp.arange(groups, dtype=jnp.int32)
    onehot = (destination[:, None] == columns[None, :]).astype(jnp.int32)
    within = jnp.cumsum(onehot.reshape(groups, per_owner, groups), axis=1).reshape(page_count, groups)
    position = lax.optimization_barrier(jnp.sum(within * onehot, axis=1)) - 1
    arrival = owner_group * capacity + position
    combined = destination * requests + request
    pair_hot = (combined[:, None] == jnp.arange(groups * requests, dtype=jnp.int32)[None, :]).astype(jnp.int32)
    running = jnp.cumsum(pair_hot, axis=0)
    page_rank = lax.optimization_barrier(jnp.sum(running * pair_hot, axis=1)) - 1
    totals = running[-1].reshape(groups, requests)
    return (position, arrival, page_rank, totals)

def alibi_slopes(head_count):
    return jnp.exp2(-8.0 * jnp.arange(1, head_count + 1).astype(jnp.float32) / head_count)

def group_attention(group_id, query, self_kv, kv_pages, destination, request, arrival, page_rank, totals, slopes):
    tok_grp = TOK_GRP
    buffer = N_GROUP * CAP
    queries = lax.dynamic_slice_in_dim(query, group_id * tok_grp, tok_grp, 1).astype(jnp.float32).reshape(2, tok_grp, HEADS, HEAD_DIM)
    own_kv = lax.dynamic_slice_in_dim(self_kv, group_id * tok_grp, tok_grp, 1).astype(jnp.float32)
    own_keys = own_kv[:, :, 0].reshape(2, tok_grp, HEADS, HEAD_DIM)
    own_values = own_kv[:, :, 1].reshape(2, tok_grp, HEADS, HEAD_DIM)
    target_place = jnp.where(destination == group_id, arrival, buffer)
    slot_index = jnp.full((buffer,), PAGES, jnp.int32).at[target_place].set(jnp.arange(PAGES, dtype=jnp.int32), mode='drop')
    is_valid = slot_index < PAGES
    safe_index = jnp.minimum(slot_index, PAGES - 1)
    page_data = kv_pages[:, safe_index].astype(jnp.float32)
    key_data = page_data[:, :, :, 0].reshape(2, buffer * PAGE, HEADS, HEAD_DIM)
    values = page_data[:, :, :, 1].reshape(2, buffer * PAGE, HEADS, HEAD_DIM)
    key_request = jnp.repeat(jnp.where(is_valid, request[safe_index], -1), PAGE)
    key_position = (page_rank[safe_index][:, None] * PAGE + jnp.arange(PAGE, dtype=jnp.int32)[None, :]).reshape(-1)
    token_ids = jnp.arange(tok_grp, dtype=jnp.int32)
    token_request = token_ids // SCORE_LEN
    token_step = token_ids % SCORE_LEN
    context = totals[group_id][token_request] * PAGE
    distance = (context + token_step)[:, None] - key_position[None, :]
    score_scale = 1.0 / math.sqrt(HEAD_DIM)
    scores = jnp.einsum('mthd,mkhd->mhtk', queries, key_data) * score_scale - slopes[None, :, None, None] * distance.astype(jnp.float32)[None, None]
    allowed = (key_request[None, :] == token_request[:, None])[None, None]
    scores = jnp.where(allowed, scores, NEGATIVE)
    own_distance = (token_step[:, None] - token_step[None, :]).astype(jnp.float32)
    own_scores = jnp.einsum('mthd,mshd->mhts', queries, own_keys) * score_scale - slopes[None, :, None, None] * own_distance[None, None]
    own_allowed = ((token_request[:, None] == token_request[None, :]) & (token_step[None, :] <= token_step[:, None]))[None, None]
    own_scores = jnp.where(own_allowed, own_scores, NEGATIVE)
    row_top = jnp.maximum(lax.optimization_barrier(jnp.max(scores, -1)), lax.optimization_barrier(jnp.max(own_scores, -1)))
    exp_terms = jnp.where(allowed, jnp.exp(scores - row_top[..., None]), 0.0)
    own_terms = jnp.where(own_allowed, jnp.exp(own_scores - row_top[..., None]), 0.0)
    denominator = lax.optimization_barrier(jnp.sum(exp_terms, -1)) + lax.optimization_barrier(jnp.sum(own_terms, -1))
    weights = lax.optimization_barrier(exp_terms.astype(jnp.bfloat16)).astype(jnp.float32)
    own_weights = lax.optimization_barrier(own_terms.astype(jnp.bfloat16)).astype(jnp.float32)
    numerator = jnp.einsum('mhtk,mkhd->mthd', weights, values) + jnp.einsum('mhts,mshd->mthd', own_weights, own_values)
    attended = numerator / jnp.transpose(denominator, (0, 2, 1))[..., None]
    return attended.reshape(2, tok_grp, HEADS * HEAD_DIM).astype(jnp.bfloat16)

def reference(query, self_kv, kv_pages, page_dest, page_request, score_len, out_proj, residual, norm_gain, norm_bias, vocab, targets):
    destination = page_dest[:, 0]
    position, arrival, page_rank, totals = route_tables(destination, page_request, N_GROUP, PAGES_DEV, CAP, REQ_GRP)
    slopes = alibi_slopes(HEADS)

    def one_group(group_id):
        return group_attention(group_id, query, self_kv, kv_pages, destination, page_request, arrival, page_rank, totals, slopes)
    blocks = lax.map(one_group, jnp.arange(N_GROUP, dtype=jnp.int32))
    attended = jnp.transpose(blocks, (1, 0, 2, 3)).reshape(2, TOKENS, HEADS * HEAD_DIM)
    hidden = residual.astype(jnp.float32) + jnp.einsum('mtk,mkd->mtd', attended.astype(jnp.float32), out_proj.astype(jnp.float32))
    row_mean = lax.optimization_barrier(jnp.mean(hidden, axis=-1, keepdims=True))
    centered = hidden - row_mean
    variance = lax.optimization_barrier(jnp.mean(centered * centered, axis=-1, keepdims=True))
    normed = (centered / jnp.sqrt(variance + EPSILON) * norm_gain[:, None, :] + norm_bias[:, None, :]).astype(jnp.bfloat16)

    def score_block(group_id):
        row_block = lax.dynamic_slice_in_dim(normed, group_id * TOK_GRP, TOK_GRP, 1)
        wanted = lax.dynamic_slice_in_dim(targets, group_id * TOK_GRP, TOK_GRP, 0)
        results = []
        for which_model in range(2):
            logits = jnp.dot(row_block[which_model], vocab[which_model], preferred_element_type=jnp.float32)
            row_peak = lax.optimization_barrier(jnp.max(logits, axis=1))
            log_total = row_peak + jnp.log(lax.optimization_barrier(jnp.sum(jnp.exp(logits - row_peak[:, None]), axis=1)))
            chosen = jnp.take_along_axis(logits, wanted[:, None], axis=1)[:, 0]
            results.append(chosen - log_total)
        return jnp.stack(results, 0)
    scored = lax.map(score_block, jnp.arange(N_GROUP, dtype=jnp.int32))
    logprob_all = jnp.transpose(scored, (1, 0, 2)).reshape(2, TOKENS)
    token_ids = jnp.arange(TOKENS, dtype=jnp.int32)
    keep_token = token_ids % SCORE_LEN < score_len[token_ids // SCORE_LEN]
    return jnp.where(keep_token[None, :], logprob_all, 0.0)
```

```python
import math

import jax
import jax.numpy as jnp
from jax import lax
from jax.sharding import PartitionSpec as P

HEADS = 16
HEAD_DIM = 128
REQ_GRP = 2
SCORE_LEN = 16


NEGATIVE = -1e30
EPSILON = 1e-05


def alibi_slopes(head_count):
    return jnp.exp2(-8.0 * jnp.arange(1, head_count + 1).astype(jnp.float32) / head_count)


def lse_combine(peak, total, chosen, axis):
    top = jnp.max(peak, axis=axis, keepdims=True)
    total = jnp.sum(total * jnp.exp(peak - top), axis=axis)
    return jnp.squeeze(top, axis), total, jnp.sum(chosen, axis=axis)


def per_device(
    query,
    self_kv,
    kv_pages,
    page_dest,
    page_request,
    score_len,
    out_proj,
    residual,
    norm_gain,
    norm_bias,
    vocab,
    targets,
):
    groups = lax.axis_size("group")
    shards = lax.axis_size("tensor")
    group_id = lax.axis_index("group")
    tensor_id = lax.axis_index("tensor")
    tok_grp = query.shape[1]
    flat_width = query.shape[2]
    head_local = flat_width // HEAD_DIM
    per_owner = kv_pages.shape[1]
    page_len = kv_pages.shape[2]
    capacity = 2 * per_owner // groups
    destination = page_dest[:, 0]
    page_total = destination.shape[0]
    buffer = groups * capacity
    width = residual.shape[2]

    local = jnp.arange(per_owner, dtype=jnp.int32)
    earlier = local[None, :] < local[:, None]
    my_dest = lax.dynamic_slice_in_dim(destination, group_id * per_owner, per_owner)
    my_position = jnp.sum(
        ((my_dest[None, :] == my_dest[:, None]) & earlier).astype(jnp.int32), axis=1
    )
    out_slot = my_dest * capacity + my_position
    slots = jnp.arange(buffer, dtype=jnp.int32)
    send_hot = out_slot[None, :] == slots[:, None]
    send_from = jnp.sum(jnp.where(send_hot, local[None, :], 0), axis=1)
    outgoing = jnp.take(kv_pages, send_from, axis=1)
    incoming = lax.all_to_all(outgoing, "group", split_axis=1, concat_axis=1, tiled=True)

    pages = jnp.arange(page_total, dtype=jnp.int32)
    mine = destination == group_id
    mine_blocks = mine.reshape(groups, per_owner)
    rank_in_block = jnp.sum(
        (mine_blocks[:, None, :] & earlier[None]).astype(jnp.int32), axis=2
    ).reshape(-1)
    arrival = (pages // per_owner) * capacity + rank_in_block
    recv_hot = mine[None, :] & (arrival[None, :] == slots[:, None])
    is_valid = jnp.any(recv_hot, axis=1)
    slot_page = jnp.sum(jnp.where(recv_hot, pages[None, :], 0), axis=1)
    slot_request = jnp.sum(jnp.where(recv_hot, page_request[None, :], 0), axis=1)
    slot_rank = jnp.sum(
        (
            mine[None, :]
            & (page_request[None, :] == slot_request[:, None])
            & (pages[None, :] < slot_page[:, None])
        ).astype(jnp.int32),
        axis=1,
    )
    request_ids = jnp.arange(REQ_GRP, dtype=jnp.int32)
    totals = jnp.sum(
        (mine[None, :] & (page_request[None, :] == request_ids[:, None])).astype(jnp.int32),
        axis=1,
    )

    slopes = lax.dynamic_slice_in_dim(alibi_slopes(HEADS), tensor_id * head_local, head_local)
    score_scale = 1.0 / math.sqrt(HEAD_DIM)
    queries = query.reshape(2, tok_grp, head_local, HEAD_DIM)
    own_keys = self_kv[:, :, 0].reshape(2, tok_grp, head_local, HEAD_DIM)
    own_values = self_kv[:, :, 1].reshape(2, tok_grp, head_local, HEAD_DIM)
    token_ids = jnp.arange(tok_grp, dtype=jnp.int32)
    token_request = token_ids // SCORE_LEN
    token_step = token_ids % SCORE_LEN
    own_distance = (token_step[:, None] - token_step[None, :]).astype(jnp.float32)
    own_scores = (
        jnp.einsum("mthd,mshd->mhts", queries, own_keys, preferred_element_type=jnp.float32)
        * score_scale
    )
    own_scores = own_scores - slopes[None, :, None, None] * own_distance[None, None]
    own_allowed = (
        (token_request[:, None] == token_request[None, :])
        & (token_step[None, :] <= token_step[:, None])
    )[None, None]
    own_scores = jnp.where(own_allowed, own_scores, NEGATIVE)
    own_top = jnp.max(own_scores, -1)

    key_data = incoming[:, :, :, 0].reshape(2, buffer * page_len, head_local, HEAD_DIM)
    values = incoming[:, :, :, 1].reshape(2, buffer * page_len, head_local, HEAD_DIM)
    key_request = jnp.repeat(jnp.where(is_valid, slot_request, -1), page_len)
    key_position = (
        slot_rank[:, None] * page_len + jnp.arange(page_len, dtype=jnp.int32)[None, :]
    ).reshape(-1)
    context = totals[token_request] * page_len
    distance = ((context + token_step)[:, None] - key_position[None, :]).astype(jnp.float32)
    scores = (
        jnp.einsum("mthd,mkhd->mhtk", queries, key_data, preferred_element_type=jnp.float32)
        * score_scale
    )
    scores = scores - slopes[None, :, None, None] * distance[None, None]
    allowed = (key_request[None, :] == token_request[:, None])[None, None]
    scores = jnp.where(allowed, scores, NEGATIVE)
    row_top = jnp.maximum(jnp.max(scores, -1), own_top)
    exp_terms = jnp.where(allowed, jnp.exp(scores - row_top[..., None]), 0.0)
    denominator = jnp.sum(exp_terms, -1)
    numerator = jnp.einsum(
        "mhtk,mkhd->mthd",
        exp_terms.astype(jnp.bfloat16),
        values,
        preferred_element_type=jnp.float32,
    )
    own_terms = jnp.where(own_allowed, jnp.exp(own_scores - row_top[..., None]), 0.0)
    denominator = denominator + jnp.sum(own_terms, -1)
    numerator = numerator + jnp.einsum(
        "mhts,mshd->mthd",
        own_terms.astype(jnp.bfloat16),
        own_values,
        preferred_element_type=jnp.float32,
    )
    attended = (
        (numerator / jnp.transpose(denominator, (0, 2, 1))[..., None])
        .reshape(2, tok_grp, flat_width)
        .astype(jnp.bfloat16)
    )

    rows_local = tok_grp // shards
    partial = jnp.einsum("mtk,mkd->tmd", attended, out_proj, preferred_element_type=jnp.float32)
    parts = lax.all_to_all(
        partial.reshape(shards, rows_local, 2, width), "tensor", 0, 0, tiled=True
    )
    mixed = jnp.sum(parts, axis=0)
    hidden = residual.astype(jnp.float32) + jnp.transpose(mixed, (1, 0, 2))
    row_mean = jnp.mean(hidden, axis=-1, keepdims=True)
    centered = hidden - row_mean
    variance = jnp.mean(centered * centered, axis=-1, keepdims=True)
    normed = (
        centered / jnp.sqrt(variance + EPSILON) * norm_gain[:, None, :] + norm_bias[:, None, :]
    ).astype(jnp.bfloat16)

    voc_local = vocab.shape[2]
    offset = (group_id * shards + tensor_id) * voc_local
    everyone = lax.all_gather(normed, ("group", "tensor"), axis=1, tiled=True)
    logits = jnp.einsum("mnd,mdv->mnv", everyone, vocab, preferred_element_type=jnp.float32)
    local_peak = jnp.max(logits, axis=2)
    local_total = jnp.sum(jnp.exp(logits - local_peak[..., None]), axis=2)
    wanted = targets - offset
    hit = jnp.arange(voc_local, dtype=jnp.int32)[None, None, :] == wanted[None, :, None]
    local_chosen = jnp.sum(jnp.where(hit, logits, 0.0), axis=2)

    stats = jnp.stack([local_peak, local_total, local_chosen]).reshape(
        3, 2, groups, shards, rows_local
    )
    stats = lax.all_to_all(stats, "tensor", 3, 3, tiled=True)
    peak, total, chosen = lse_combine(stats[0], stats[1], stats[2], 2)
    stats = lax.all_to_all(jnp.stack([peak, total, chosen]), "group", 2, 2, tiled=True)
    peak, total, chosen = lse_combine(stats[0], stats[1], stats[2], 1)
    mine_lp = chosen - (peak + jnp.log(total))

    local_ids = tensor_id * rows_local + jnp.arange(rows_local, dtype=jnp.int32)
    keep_token = local_ids % SCORE_LEN < score_len[local_ids // SCORE_LEN]
    return jnp.where(keep_token[None, :], mine_lp, 0.0)


def solution(mesh):
    in_specs = (
        P(None, "group", "tensor"),
        P(None, "group", None, "tensor"),
        P(None, "group", None, None, "tensor"),
        P(),
        P(),
        P("group"),
        P(None, "tensor", None),
        P(None, ("group", "tensor"), None),
        P(),
        P(),
        P(None, None, ("group", "tensor")),
        P(),
    )
    out_specs = P(None, ("group", "tensor"))
    return jax.shard_map(
        per_device, mesh=mesh, in_specs=in_specs, out_specs=out_specs, check_vma=False
    )
```

```python
import math

import jax
import jax.numpy as jnp
from jax import lax
from jax.sharding import PartitionSpec as P

HEADS = 16
HEAD_DIM = 128
REQ_GRP = 2
SCORE_LEN = 16


NEGATIVE = -1e30
EPSILON = 1e-05


def alibi_slopes(head_count):
    return jnp.exp2(-8.0 * jnp.arange(1, head_count + 1).astype(jnp.float32) / head_count)


def lse_combine(peak, total, chosen, axis):
    top = jnp.max(peak, axis=axis, keepdims=True)
    total = jnp.sum(total * jnp.exp(peak - top), axis=axis)
    return jnp.squeeze(top, axis), total, jnp.sum(chosen, axis=axis)


def per_device(
    query,
    self_kv,
    kv_pages,
    page_dest,
    page_request,
    score_len,
    out_proj,
    residual,
    norm_gain,
    norm_bias,
    vocab,
    targets,
):
    groups = lax.axis_size("group")
    shards = lax.axis_size("tensor")
    group_id = lax.axis_index("group")
    tensor_id = lax.axis_index("tensor")
    tok_grp = query.shape[1]
    flat_width = query.shape[2]
    head_local = flat_width // HEAD_DIM
    per_owner = kv_pages.shape[1]
    page_len = kv_pages.shape[2]
    capacity = 2 * per_owner // groups
    destination = page_dest[:, 0]
    page_total = destination.shape[0]
    buffer = groups * capacity
    width = residual.shape[2]

    local = jnp.arange(per_owner, dtype=jnp.int32)
    earlier = local[None, :] < local[:, None]
    my_dest = lax.dynamic_slice_in_dim(destination, group_id * per_owner, per_owner)
    my_position = jnp.sum(
        ((my_dest[None, :] == my_dest[:, None]) & earlier).astype(jnp.int32), axis=1
    )
    out_slot = my_dest * capacity + my_position
    slots = jnp.arange(buffer, dtype=jnp.int32)
    send_hot = (out_slot[None, :] == slots[:, None]).astype(kv_pages.dtype)
    outgoing = jnp.einsum(
        "sp,mpjcx->cmsjx", send_hot, kv_pages, preferred_element_type=jnp.float32
    ).astype(kv_pages.dtype)
    incoming = lax.all_to_all(outgoing, "group", split_axis=2, concat_axis=2, tiled=True)

    pages = jnp.arange(page_total, dtype=jnp.int32)
    mine = destination == group_id
    mine_blocks = mine.reshape(groups, per_owner)
    rank_in_block = jnp.sum(
        (mine_blocks[:, None, :] & earlier[None]).astype(jnp.int32), axis=2
    ).reshape(-1)
    arrival = (pages // per_owner) * capacity + rank_in_block
    recv_hot = mine[None, :] & (arrival[None, :] == slots[:, None])
    is_valid = jnp.any(recv_hot, axis=1)
    slot_page = jnp.sum(jnp.where(recv_hot, pages[None, :], 0), axis=1)
    slot_request = jnp.sum(jnp.where(recv_hot, page_request[None, :], 0), axis=1)
    slot_rank = jnp.sum(
        (
            mine[None, :]
            & (page_request[None, :] == slot_request[:, None])
            & (pages[None, :] < slot_page[:, None])
        ).astype(jnp.int32),
        axis=1,
    )
    request_ids = jnp.arange(REQ_GRP, dtype=jnp.int32)
    totals = jnp.sum(
        (mine[None, :] & (page_request[None, :] == request_ids[:, None])).astype(jnp.int32),
        axis=1,
    )

    slopes = lax.dynamic_slice_in_dim(alibi_slopes(HEADS), tensor_id * head_local, head_local)
    score_scale = 1.0 / math.sqrt(HEAD_DIM)
    queries = query.reshape(2, tok_grp, head_local, HEAD_DIM)
    own_keys = self_kv[:, :, 0].reshape(2, tok_grp, head_local, HEAD_DIM)
    own_values = self_kv[:, :, 1].reshape(2, tok_grp, head_local, HEAD_DIM)
    token_ids = jnp.arange(tok_grp, dtype=jnp.int32)
    token_request = token_ids // SCORE_LEN
    token_step = token_ids % SCORE_LEN
    own_distance = (token_step[:, None] - token_step[None, :]).astype(jnp.float32)
    own_scores = (
        jnp.einsum("mthd,mshd->mhts", queries, own_keys, preferred_element_type=jnp.float32)
        * score_scale
    )
    own_scores = own_scores - slopes[None, :, None, None] * own_distance[None, None]
    own_allowed = (
        (token_request[:, None] == token_request[None, :])
        & (token_step[None, :] <= token_step[:, None])
    )[None, None]
    own_scores = jnp.where(own_allowed, own_scores, NEGATIVE)
    own_top = jnp.max(own_scores, -1)

    key_data = incoming[0].reshape(2, buffer * page_len, head_local, HEAD_DIM)
    values = incoming[1].reshape(2, buffer * page_len, head_local, HEAD_DIM)
    key_request = jnp.repeat(jnp.where(is_valid, slot_request, -1), page_len)
    key_position = (
        slot_rank[:, None] * page_len + jnp.arange(page_len, dtype=jnp.int32)[None, :]
    ).reshape(-1)
    context = totals[token_request] * page_len
    distance = ((context + token_step)[:, None] - key_position[None, :]).astype(jnp.float32)
    scores = (
        jnp.einsum("mthd,mkhd->mhtk", queries, key_data, preferred_element_type=jnp.float32)
        * score_scale
    )
    scores = scores - slopes[None, :, None, None] * distance[None, None]
    allowed = (key_request[None, :] == token_request[:, None])[None, None]
    scores = jnp.where(allowed, scores, NEGATIVE)
    row_top = jnp.maximum(jnp.max(scores, -1), own_top)
    exp_terms = jnp.where(allowed, jnp.exp(scores - row_top[..., None]), 0.0)
    denominator = jnp.sum(exp_terms, -1)
    numerator = jnp.einsum(
        "mhtk,mkhd->mthd",
        exp_terms.astype(jnp.bfloat16),
        values,
        preferred_element_type=jnp.float32,
    )
    own_terms = jnp.where(own_allowed, jnp.exp(own_scores - row_top[..., None]), 0.0)
    denominator = denominator + jnp.sum(own_terms, -1)
    numerator = numerator + jnp.einsum(
        "mhts,mshd->mthd",
        own_terms.astype(jnp.bfloat16),
        own_values,
        preferred_element_type=jnp.float32,
    )
    attended = (
        (numerator / jnp.transpose(denominator, (0, 2, 1))[..., None])
        .reshape(2, tok_grp, flat_width)
        .astype(jnp.bfloat16)
    )

    rows_local = tok_grp // shards
    partial = jnp.einsum("mtk,mkd->tmd", attended, out_proj, preferred_element_type=jnp.float32)
    parts = lax.all_to_all(
        partial.reshape(shards, rows_local, 2, width), "tensor", 0, 0, tiled=True
    )
    mixed = jnp.sum(parts, axis=0)
    hidden = residual.astype(jnp.float32) + jnp.transpose(mixed, (1, 0, 2))
    row_mean = jnp.mean(hidden, axis=-1, keepdims=True)
    centered = hidden - row_mean
    variance = jnp.mean(centered * centered, axis=-1, keepdims=True)
    normed = (
        centered / jnp.sqrt(variance + EPSILON) * norm_gain[:, None, :] + norm_bias[:, None, :]
    ).astype(jnp.bfloat16)

    voc_local = vocab.shape[2]
    offset = (group_id * shards + tensor_id) * voc_local
    side = tensor_id % 2
    y_size = 4
    z_size = groups // y_size
    z_id = group_id // y_size
    y_id = group_id % y_size
    block = lax.all_gather(normed, "tensor", axis=0, tiled=False)
    block = lax.dynamic_index_in_dim(block, side, 1, keepdims=False)

    def y_shift(step):
        return [(z * y_size + y, z * y_size + (y + step) % y_size)
                for z in range(z_size) for y in range(y_size)]

    def z_shift(step):
        return [(z * y_size + y, ((z + step) % z_size) * y_size + y)
                for z in range(z_size) for y in range(y_size)]

    block = jnp.stack([block] + [lax.ppermute(block, "group", y_shift(k)) for k in range(1, y_size)])
    forward, backward = block, block
    chunks = [block]
    z_from = [0]
    for k in range(1, z_size // 2 + 1):
        forward = lax.ppermute(forward, "group", z_shift(1))
        chunks.append(forward)
        z_from.append(k)
        if k < z_size // 2:
            backward = lax.ppermute(backward, "group", z_shift(z_size - 1))
            chunks.append(backward)
            z_from.append(z_size - k)
    own_model = jnp.stack(chunks)
    other_model = lax.ppermute(
        own_model, "tensor", [(t, t ^ 1) for t in range(shards)]
    )
    z_from = jnp.array(z_from, dtype=jnp.int32)
    y_from = jnp.arange(y_size, dtype=jnp.int32)
    source_group = (
        ((z_id - z_from[:, None]) % z_size) * y_size + (y_id - y_from[None, :]) % y_size
    ).reshape(-1)
    token_rows = shards * rows_local
    wanted = (targets.reshape(groups, token_rows)[source_group] - offset).reshape(-1)
    lanes = jnp.arange(voc_local, dtype=jnp.int32)

    def local_stats(rows, weights):
        logits = jnp.dot(rows.reshape(-1, width), weights, preferred_element_type=jnp.float32)
        peak = jnp.max(logits, axis=1)
        total = jnp.sum(jnp.exp(logits - peak[:, None]), axis=1)
        chosen = jnp.sum(jnp.where(lanes[None, :] == wanted[:, None], logits, 0.0), axis=1)
        return jnp.stack([peak, total, chosen])

    own_stats = local_stats(own_model, lax.dynamic_index_in_dim(vocab, side, 0, keepdims=False))
    other_stats = local_stats(
        other_model, lax.dynamic_index_in_dim(vocab, 1 - side, 0, keepdims=False)
    )
    stats = jnp.where(
        side == 0, jnp.stack([own_stats, other_stats], 1), jnp.stack([other_stats, own_stats], 1)
    ).reshape(3, 2, groups, token_rows)
    inverse = jnp.zeros((groups,), jnp.int32).at[source_group].set(
        jnp.arange(groups, dtype=jnp.int32)
    )
    stats = jnp.take(stats, inverse, axis=2).reshape(3, 2, groups, shards, rows_local)

    stats = lax.all_to_all(stats, "tensor", 3, 3, tiled=True)
    peak, total, chosen = lse_combine(stats[0], stats[1], stats[2], 2)
    stats = lax.all_to_all(jnp.stack([peak, total, chosen]), "group", 2, 2, tiled=True)
    peak, total, chosen = lse_combine(stats[0], stats[1], stats[2], 1)
    mine_lp = chosen - (peak + jnp.log(total))

    local_ids = tensor_id * rows_local + jnp.arange(rows_local, dtype=jnp.int32)
    keep_token = local_ids % SCORE_LEN < score_len[local_ids // SCORE_LEN]
    return jnp.where(keep_token[None, :], mine_lp, 0.0)


def solution(mesh):
    in_specs = (
        P(None, "group", "tensor"),
        P(None, "group", None, "tensor"),
        P(None, "group", None, None, "tensor"),
        P(),
        P(),
        P("group"),
        P(None, "tensor", None),
        P(None, ("group", "tensor"), None),
        P(),
        P(),
        P(None, None, ("group", "tensor")),
        P(),
    )
    out_specs = P(None, ("group", "tensor"))
    return jax.shard_map(
        per_device, mesh=mesh, in_specs=in_specs, out_specs=out_specs, check_vma=False
    )
```

```python
import math

import jax
import jax.numpy as jnp
from jax import lax
from jax.sharding import PartitionSpec as P

HEADS = 16
HEAD_DIM = 128
REQ_GRP = 2
SCORE_LEN = 16


NEGATIVE = -1e30
EPSILON = 1e-05


def alibi_slopes(head_count):
    return jnp.exp2(-8.0 * jnp.arange(1, head_count + 1).astype(jnp.float32) / head_count)


def lse_combine(peak, total, chosen, axis):
    top = jnp.max(peak, axis=axis, keepdims=True)
    total = jnp.sum(total * jnp.exp(peak - top), axis=axis)
    return jnp.squeeze(top, axis), total, jnp.sum(chosen, axis=axis)


def per_device(
    query,
    self_kv,
    kv_pages,
    page_dest,
    page_request,
    score_len,
    out_proj,
    residual,
    norm_gain,
    norm_bias,
    vocab,
    targets,
):
    groups = lax.axis_size("group")
    shards = lax.axis_size("tensor")
    group_id = lax.axis_index("group")
    tensor_id = lax.axis_index("tensor")
    tok_grp = query.shape[1]
    flat_width = query.shape[2]
    head_local = flat_width // HEAD_DIM
    per_owner = kv_pages.shape[1]
    page_len = kv_pages.shape[2]
    capacity = 2 * per_owner // groups
    destination = page_dest[:, 0]
    page_total = destination.shape[0]
    buffer = groups * capacity
    width = residual.shape[2]

    local = jnp.arange(per_owner, dtype=jnp.int32)
    earlier = local[None, :] < local[:, None]
    my_dest = lax.dynamic_slice_in_dim(destination, group_id * per_owner, per_owner)
    my_position = jnp.sum(
        ((my_dest[None, :] == my_dest[:, None]) & earlier).astype(jnp.int32), axis=1
    )
    out_slot = my_dest * capacity + my_position
    slots = jnp.arange(buffer, dtype=jnp.int32)
    send_hot = (out_slot[None, :] == slots[:, None]).astype(kv_pages.dtype)
    outgoing = jnp.einsum(
        "sp,mpjcx->cmsjx", send_hot, kv_pages, preferred_element_type=jnp.float32
    ).astype(kv_pages.dtype)
    incoming = lax.all_to_all(outgoing, "group", split_axis=2, concat_axis=2, tiled=True)

    pages = jnp.arange(page_total, dtype=jnp.int32)
    mine = destination == group_id
    mine_blocks = mine.reshape(groups, per_owner)
    rank_in_block = jnp.sum(
        (mine_blocks[:, None, :] & earlier[None]).astype(jnp.int32), axis=2
    ).reshape(-1)
    arrival = (pages // per_owner) * capacity + rank_in_block
    recv_hot = mine[None, :] & (arrival[None, :] == slots[:, None])
    is_valid = jnp.any(recv_hot, axis=1)
    slot_page = jnp.sum(jnp.where(recv_hot, pages[None, :], 0), axis=1)
    slot_request = jnp.sum(jnp.where(recv_hot, page_request[None, :], 0), axis=1)
    slot_rank = jnp.sum(
        (
            mine[None, :]
            & (page_request[None, :] == slot_request[:, None])
            & (pages[None, :] < slot_page[:, None])
        ).astype(jnp.int32),
        axis=1,
    )
    request_ids = jnp.arange(REQ_GRP, dtype=jnp.int32)
    totals = jnp.sum(
        (mine[None, :] & (page_request[None, :] == request_ids[:, None])).astype(jnp.int32),
        axis=1,
    )

    slopes = lax.dynamic_slice_in_dim(alibi_slopes(HEADS), tensor_id * head_local, head_local)
    score_scale = 1.0 / math.sqrt(HEAD_DIM)
    token_ids = jnp.arange(tok_grp, dtype=jnp.int32)
    token_request = token_ids // SCORE_LEN
    token_step = token_ids % SCORE_LEN
    own_distance = (token_step[:, None] - token_step[None, :]).astype(jnp.float32)
    own_allowed = (
        (token_request[:, None] == token_request[None, :])
        & (token_step[None, :] <= token_step[:, None])
    )[None]
    key_request = jnp.repeat(jnp.where(is_valid, slot_request, -1), page_len)
    key_position = (
        slot_rank[:, None] * page_len + jnp.arange(page_len, dtype=jnp.int32)[None, :]
    ).reshape(-1)
    context = totals[token_request] * page_len
    distance = ((context + token_step)[:, None] - key_position[None, :]).astype(jnp.float32)
    allowed = (key_request[None, :] == token_request[:, None])[None]
    page_keys = incoming[0].reshape(2, buffer * page_len, flat_width)
    page_values = incoming[1].reshape(2, buffer * page_len, flat_width)
    heads_out = []
    for h in range(head_local):
        lanes_h = slice(h * HEAD_DIM, (h + 1) * HEAD_DIM)
        q = query[:, :, lanes_h]
        own_k = self_kv[:, :, 0, lanes_h]
        own_v = self_kv[:, :, 1, lanes_h]
        slope = slopes[h]
        own_scores = (
            jnp.einsum("mtd,msd->mts", q, own_k, preferred_element_type=jnp.float32) * score_scale
        )
        own_scores = own_scores - slope * own_distance[None]
        own_scores = jnp.where(own_allowed, own_scores, NEGATIVE)
        scores = (
            jnp.einsum("mtd,mkd->mtk", q, page_keys[:, :, lanes_h],
                       preferred_element_type=jnp.float32) * score_scale
        )
        scores = scores - slope * distance[None]
        scores = jnp.where(allowed, scores, NEGATIVE)
        row_top = jnp.maximum(jnp.max(scores, -1), jnp.max(own_scores, -1))
        exp_terms = jnp.where(allowed, jnp.exp(scores - row_top[..., None]), 0.0)
        own_terms = jnp.where(own_allowed, jnp.exp(own_scores - row_top[..., None]), 0.0)
        denominator = jnp.sum(exp_terms, -1) + jnp.sum(own_terms, -1)
        numerator = jnp.einsum(
            "mtk,mkd->mtd", exp_terms.astype(jnp.bfloat16), page_values[:, :, lanes_h],
            preferred_element_type=jnp.float32,
        ) + jnp.einsum(
            "mts,msd->mtd", own_terms.astype(jnp.bfloat16), own_v,
            preferred_element_type=jnp.float32,
        )
        heads_out.append(numerator / denominator[..., None])
    attended = jnp.concatenate(heads_out, axis=-1).astype(jnp.bfloat16)

    rows_local = tok_grp // shards
    partial = jnp.einsum("mtk,mkd->tmd", attended, out_proj, preferred_element_type=jnp.float32)
    parts = lax.all_to_all(
        partial.reshape(shards, rows_local, 2, width), "tensor", 0, 0, tiled=True
    )
    mixed = jnp.sum(parts, axis=0)
    hidden = residual.astype(jnp.float32) + jnp.transpose(mixed, (1, 0, 2))
    row_mean = jnp.mean(hidden, axis=-1, keepdims=True)
    centered = hidden - row_mean
    variance = jnp.mean(centered * centered, axis=-1, keepdims=True)
    normed = (
        centered / jnp.sqrt(variance + EPSILON) * norm_gain[:, None, :] + norm_bias[:, None, :]
    ).astype(jnp.bfloat16)

    voc_local = vocab.shape[2]
    offset = (group_id * shards + tensor_id) * voc_local
    side = tensor_id % 2
    x_size = shards // 2
    x_id = tensor_id // 2
    y_size = 4
    z_size = groups // y_size
    z_id = group_id // y_size
    y_id = group_id % y_size
    swap = [(t, t ^ 1) for t in range(shards)]
    kept = lax.dynamic_index_in_dim(normed, side, 0, keepdims=False)
    given = lax.ppermute(lax.dynamic_index_in_dim(normed, 1 - side, 0, keepdims=False), "tensor", swap)
    block = jnp.where(
        side == 0, jnp.concatenate([kept, given], 0), jnp.concatenate([given, kept], 0)
    )

    def x_shift(step):
        return [(t, (t + 2 * step) % shards) for t in range(shards)]

    def y_shift(step):
        return [(z * y_size + y, z * y_size + (y + step) % y_size)
                for z in range(z_size) for y in range(y_size)]

    def z_shift(step):
        return [(z * y_size + y, ((z + step) % z_size) * y_size + y)
                for z in range(z_size) for y in range(y_size)]

    block = jnp.concatenate(
        [block] + [lax.ppermute(block, "tensor", x_shift(k)) for k in range(1, x_size)], 0
    )
    block = jnp.concatenate(
        [block] + [lax.ppermute(block, "group", y_shift(k)) for k in range(1, y_size)], 0
    )
    forward, backward = block, block
    chunks = [block]
    z_from = [0]
    for k in range(1, z_size // 2 + 1):
        forward = lax.ppermute(forward, "group", z_shift(1))
        chunks.append(forward)
        z_from.append(k)
        if k < z_size // 2:
            backward = lax.ppermute(backward, "group", z_shift(z_size - 1))
            chunks.append(backward)
            z_from.append(z_size - k)
    own_model = jnp.concatenate(chunks, 0)
    other_model = lax.ppermute(own_model, "tensor", swap)
    z_from = jnp.array(z_from, dtype=jnp.int32)
    y_from = jnp.arange(y_size, dtype=jnp.int32)
    source_group = (
        ((z_id - z_from[:, None]) % z_size) * y_size + (y_id - y_from[None, :]) % y_size
    ).reshape(-1)
    x_from = (x_id - jnp.arange(x_size, dtype=jnp.int32)) % x_size
    pair_rows = 2 * rows_local
    wanted = (
        targets.reshape(groups, x_size, pair_rows)[source_group[:, None], x_from[None, :]] - offset
    ).reshape(-1)
    lanes = jnp.arange(voc_local, dtype=jnp.int32)

    def local_stats(rows, weights):
        logits = jnp.dot(rows, weights, preferred_element_type=jnp.float32)
        peak = jnp.max(logits, axis=1)
        total = jnp.sum(jnp.exp(logits - peak[:, None]), axis=1)
        chosen = jnp.sum(jnp.where(lanes[None, :] == wanted[:, None], logits, 0.0), axis=1)
        return jnp.stack([peak, total, chosen])

    own_stats = local_stats(own_model, lax.dynamic_index_in_dim(vocab, side, 0, keepdims=False))
    other_stats = local_stats(
        other_model, lax.dynamic_index_in_dim(vocab, 1 - side, 0, keepdims=False)
    )
    stats = jnp.where(
        side == 0, jnp.stack([own_stats, other_stats], 1), jnp.stack([other_stats, own_stats], 1)
    ).reshape(3, 2, groups, x_size, pair_rows)
    group_at = jnp.zeros((groups,), jnp.int32).at[source_group].set(
        jnp.arange(groups, dtype=jnp.int32)
    )
    x_at = (x_id - jnp.arange(x_size, dtype=jnp.int32)) % x_size
    stats = jnp.take(jnp.take(stats, group_at, axis=2), x_at, axis=3)
    stats = stats.reshape(3, 2, groups, shards, rows_local)

    stats = lax.all_to_all(stats, "tensor", 3, 3, tiled=True)
    peak, total, chosen = lse_combine(stats[0], stats[1], stats[2], 2)
    stats = lax.all_to_all(jnp.stack([peak, total, chosen]), "group", 2, 2, tiled=True)
    peak, total, chosen = lse_combine(stats[0], stats[1], stats[2], 1)
    mine_lp = chosen - (peak + jnp.log(total))

    local_ids = tensor_id * rows_local + jnp.arange(rows_local, dtype=jnp.int32)
    keep_token = local_ids % SCORE_LEN < score_len[local_ids // SCORE_LEN]
    return jnp.where(keep_token[None, :], mine_lp, 0.0)


def solution(mesh):
    in_specs = (
        P(None, "group", "tensor"),
        P(None, "group", None, "tensor"),
        P(None, "group", None, None, "tensor"),
        P(),
        P(),
        P("group"),
        P(None, "tensor", None),
        P(None, ("group", "tensor"), None),
        P(),
        P(),
        P(None, None, ("group", "tensor")),
        P(),
    )
    out_specs = P(None, ("group", "tensor"))
    return jax.shard_map(
        per_device, mesh=mesh, in_specs=in_specs, out_specs=out_specs, check_vma=False
    )
```

```python
import math

import jax
import jax.numpy as jnp
from jax import lax
from jax.sharding import PartitionSpec as P

HEADS = 16
HEAD_DIM = 128
REQ_GRP = 2
SCORE_LEN = 16


NEGATIVE = -1e30
EPSILON = 1e-05


def alibi_slopes(head_count):
    return jnp.exp2(-8.0 * jnp.arange(1, head_count + 1).astype(jnp.float32) / head_count)


def lse_combine(peak, total, chosen, axis):
    top = jnp.max(peak, axis=axis, keepdims=True)
    total = jnp.sum(total * jnp.exp(peak - top), axis=axis)
    return jnp.squeeze(top, axis), total, jnp.sum(chosen, axis=axis)


def per_device(
    query,
    self_kv,
    kv_pages,
    page_dest,
    page_request,
    score_len,
    out_proj,
    residual,
    norm_gain,
    norm_bias,
    vocab,
    targets,
):
    groups = lax.axis_size("group")
    shards = lax.axis_size("tensor")
    group_id = lax.axis_index("group")
    tensor_id = lax.axis_index("tensor")
    tok_grp = query.shape[1]
    flat_width = query.shape[2]
    head_local = flat_width // HEAD_DIM
    per_owner = kv_pages.shape[1]
    page_len = kv_pages.shape[2]
    capacity = 2 * per_owner // groups
    destination = page_dest[:, 0]
    page_total = destination.shape[0]
    buffer = groups * capacity
    width = residual.shape[2]

    local = jnp.arange(per_owner, dtype=jnp.int32)
    earlier = local[None, :] < local[:, None]
    my_dest = lax.dynamic_slice_in_dim(destination, group_id * per_owner, per_owner)
    my_position = jnp.sum(
        ((my_dest[None, :] == my_dest[:, None]) & earlier).astype(jnp.int32), axis=1
    )
    out_slot = my_dest * capacity + my_position
    slots = jnp.arange(buffer, dtype=jnp.int32)
    send_hot = (out_slot[None, :] == slots[:, None]).astype(kv_pages.dtype)
    outgoing = jnp.einsum(
        "sp,mpjcx->cmsjx", send_hot, kv_pages, preferred_element_type=jnp.float32
    ).astype(kv_pages.dtype)
    incoming = lax.all_to_all(outgoing, "group", split_axis=2, concat_axis=2, tiled=True)

    pages = jnp.arange(page_total, dtype=jnp.int32)
    mine = destination == group_id
    mine_blocks = mine.reshape(groups, per_owner)
    rank_in_block = jnp.sum(
        (mine_blocks[:, None, :] & earlier[None]).astype(jnp.int32), axis=2
    ).reshape(-1)
    arrival = (pages // per_owner) * capacity + rank_in_block
    recv_hot = mine[None, :] & (arrival[None, :] == slots[:, None])
    is_valid = jnp.any(recv_hot, axis=1)
    slot_page = jnp.sum(jnp.where(recv_hot, pages[None, :], 0), axis=1)
    slot_request = jnp.sum(jnp.where(recv_hot, page_request[None, :], 0), axis=1)
    slot_rank = jnp.sum(
        (
            mine[None, :]
            & (page_request[None, :] == slot_request[:, None])
            & (pages[None, :] < slot_page[:, None])
        ).astype(jnp.int32),
        axis=1,
    )
    request_ids = jnp.arange(REQ_GRP, dtype=jnp.int32)
    totals = jnp.sum(
        (mine[None, :] & (page_request[None, :] == request_ids[:, None])).astype(jnp.int32),
        axis=1,
    )

    slopes = lax.dynamic_slice_in_dim(alibi_slopes(HEADS), tensor_id * head_local, head_local)
    score_scale = 1.0 / math.sqrt(HEAD_DIM)
    token_ids = jnp.arange(tok_grp, dtype=jnp.int32)
    token_request = token_ids // SCORE_LEN
    token_step = token_ids % SCORE_LEN
    own_distance = (token_step[:, None] - token_step[None, :]).astype(jnp.float32)
    own_allowed = (
        (token_request[:, None] == token_request[None, :])
        & (token_step[None, :] <= token_step[:, None])
    )[None]
    key_request = jnp.repeat(jnp.where(is_valid, slot_request, -1), page_len)
    key_position = (
        slot_rank[:, None] * page_len + jnp.arange(page_len, dtype=jnp.int32)[None, :]
    ).reshape(-1)
    context = totals[token_request] * page_len
    distance = ((context + token_step)[:, None] - key_position[None, :]).astype(jnp.float32)
    allowed = (key_request[None, :] == token_request[:, None])[None]
    page_keys = incoming[0].reshape(2, buffer * page_len, flat_width)
    page_values = incoming[1].reshape(2, buffer * page_len, flat_width)
    heads_out = []
    for h in range(head_local):
        lanes_h = slice(h * HEAD_DIM, (h + 1) * HEAD_DIM)
        q = query[:, :, lanes_h]
        own_k = self_kv[:, :, 0, lanes_h]
        own_v = self_kv[:, :, 1, lanes_h]
        slope = slopes[h]
        own_scores = (
            jnp.einsum("mtd,msd->mts", q, own_k, preferred_element_type=jnp.float32) * score_scale
        )
        own_scores = own_scores - slope * own_distance[None]
        own_scores = jnp.where(own_allowed, own_scores, NEGATIVE)
        scores = (
            jnp.einsum("mtd,mkd->mtk", q, page_keys[:, :, lanes_h],
                       preferred_element_type=jnp.float32) * score_scale
        )
        scores = scores - slope * distance[None]
        scores = jnp.where(allowed, scores, NEGATIVE)
        row_top = jnp.maximum(jnp.max(scores, -1), jnp.max(own_scores, -1))
        exp_terms = jnp.where(allowed, jnp.exp(scores - row_top[..., None]), 0.0)
        own_terms = jnp.where(own_allowed, jnp.exp(own_scores - row_top[..., None]), 0.0)
        denominator = jnp.sum(exp_terms, -1) + jnp.sum(own_terms, -1)
        numerator = jnp.einsum(
            "mtk,mkd->mtd", exp_terms.astype(jnp.bfloat16), page_values[:, :, lanes_h],
            preferred_element_type=jnp.float32,
        ) + jnp.einsum(
            "mts,msd->mtd", own_terms.astype(jnp.bfloat16), own_v,
            preferred_element_type=jnp.float32,
        )
        heads_out.append(numerator / denominator[..., None])
    attended = jnp.concatenate(heads_out, axis=-1).astype(jnp.bfloat16)

    rows_local = tok_grp // shards
    partial = jnp.einsum("mtk,mkd->tmd", attended, out_proj, preferred_element_type=jnp.float32)
    parts = lax.all_to_all(
        partial.reshape(shards, rows_local, 2, width), "tensor", 0, 0, tiled=True
    )
    mixed = jnp.sum(parts, axis=0)
    hidden = residual.astype(jnp.float32) + jnp.transpose(mixed, (1, 0, 2))
    row_mean = jnp.mean(hidden, axis=-1, keepdims=True)
    centered = hidden - row_mean
    variance = jnp.mean(centered * centered, axis=-1, keepdims=True)
    normed = (
        centered / jnp.sqrt(variance + EPSILON) * norm_gain[:, None, :] + norm_bias[:, None, :]
    ).astype(jnp.bfloat16)

    voc_local = vocab.shape[2]
    offset = (group_id * shards + tensor_id) * voc_local
    side = tensor_id % 2
    x_size = shards // 2
    x_id = tensor_id // 2
    y_size = 4
    z_size = groups // y_size
    z_id = group_id // y_size
    y_id = group_id % y_size
    swap = [(t, t ^ 1) for t in range(shards)]
    kept = lax.dynamic_index_in_dim(normed, side, 0, keepdims=False)
    given = lax.ppermute(lax.dynamic_index_in_dim(normed, 1 - side, 0, keepdims=False), "tensor", swap)
    block = jnp.where(
        side == 0, jnp.concatenate([kept, given], 0), jnp.concatenate([given, kept], 0)
    )

    def x_shift(step):
        return [(t, (t + 2 * step) % shards) for t in range(shards)]

    def y_shift(step):
        return [(z * y_size + y, z * y_size + (y + step) % y_size)
                for z in range(z_size) for y in range(y_size)]

    def z_shift(step):
        return [(z * y_size + y, ((z + step) % z_size) * y_size + y)
                for z in range(z_size) for y in range(y_size)]

    block = jnp.concatenate(
        [block] + [lax.ppermute(block, "tensor", x_shift(k)) for k in range(1, x_size)], 0
    )
    z_from = [0]
    for k in range(1, z_size // 2 + 1):
        z_from.append(k)
        if k < z_size // 2:
            z_from.append(z_size - k)

    def z_ring(piece):
        forward, backward = piece, piece
        chunks = [piece]
        for k in range(1, z_size // 2 + 1):
            forward = lax.ppermute(forward, "group", z_shift(1))
            chunks.append(forward)
            if k < z_size // 2:
                backward = lax.ppermute(backward, "group", z_shift(z_size - 1))
                chunks.append(backward)
        return chunks

    half = width // 2
    part = block[:, :half]
    part = jnp.concatenate(
        [part] + [lax.ppermute(part, "group", y_shift(k)) for k in range(1, y_size)], 0
    )
    first_half = jnp.concatenate(z_ring(part), 0)
    part = jnp.stack(z_ring(block[:, half:]), 0)
    second_half = jnp.stack(
        [part] + [lax.ppermute(part, "group", y_shift(k)) for k in range(1, y_size)], 1
    ).reshape(first_half.shape)
    own_model = jnp.concatenate([first_half, second_half], 1)
    other_model = lax.ppermute(own_model, "tensor", swap)
    z_from = jnp.array(z_from, dtype=jnp.int32)
    y_from = jnp.arange(y_size, dtype=jnp.int32)
    source_group = (
        ((z_id - z_from[:, None]) % z_size) * y_size + (y_id - y_from[None, :]) % y_size
    ).reshape(-1)
    x_from = (x_id - jnp.arange(x_size, dtype=jnp.int32)) % x_size
    pair_rows = 2 * rows_local
    wanted = (
        targets.reshape(groups, x_size, pair_rows)[source_group[:, None], x_from[None, :]] - offset
    ).reshape(-1)
    lanes = jnp.arange(voc_local, dtype=jnp.int32)

    def local_stats(rows, weights):
        logits = jnp.dot(rows, weights, preferred_element_type=jnp.float32)
        peak = jnp.max(logits, axis=1)
        total = jnp.sum(jnp.exp(logits - peak[:, None]), axis=1)
        chosen = jnp.sum(jnp.where(lanes[None, :] == wanted[:, None], logits, 0.0), axis=1)
        return jnp.stack([peak, total, chosen])

    own_stats = local_stats(own_model, lax.dynamic_index_in_dim(vocab, side, 0, keepdims=False))
    other_stats = local_stats(
        other_model, lax.dynamic_index_in_dim(vocab, 1 - side, 0, keepdims=False)
    )
    stats = jnp.where(
        side == 0, jnp.stack([own_stats, other_stats], 1), jnp.stack([other_stats, own_stats], 1)
    ).reshape(3, 2, groups, x_size, pair_rows)
    group_at = jnp.zeros((groups,), jnp.int32).at[source_group].set(
        jnp.arange(groups, dtype=jnp.int32)
    )
    x_at = (x_id - jnp.arange(x_size, dtype=jnp.int32)) % x_size
    stats = jnp.take(jnp.take(stats, group_at, axis=2), x_at, axis=3)
    stats = stats.reshape(3, 2, groups, shards, rows_local)

    stats = lax.all_to_all(stats, "tensor", 3, 3, tiled=True)
    peak, total, chosen = lse_combine(stats[0], stats[1], stats[2], 2)
    stats = lax.all_to_all(jnp.stack([peak, total, chosen]), "group", 2, 2, tiled=True)
    peak, total, chosen = lse_combine(stats[0], stats[1], stats[2], 1)
    mine_lp = chosen - (peak + jnp.log(total))

    local_ids = tensor_id * rows_local + jnp.arange(rows_local, dtype=jnp.int32)
    keep_token = local_ids % SCORE_LEN < score_len[local_ids // SCORE_LEN]
    return jnp.where(keep_token[None, :], mine_lp, 0.0)


def solution(mesh):
    in_specs = (
        P(None, "group", "tensor"),
        P(None, "group", None, "tensor"),
        P(None, "group", None, None, "tensor"),
        P(),
        P(),
        P("group"),
        P(None, "tensor", None),
        P(None, ("group", "tensor"), None),
        P(),
        P(),
        P(None, None, ("group", "tensor")),
        P(),
    )
    out_specs = P(None, ("group", "tensor"))
    return jax.shard_map(
        per_device, mesh=mesh, in_specs=in_specs, out_specs=out_specs, check_vma=False
    )
```

```python
import math

import jax
import jax.numpy as jnp
from jax import lax
from jax.sharding import PartitionSpec as P

HEADS = 16
HEAD_DIM = 128
REQ_GRP = 2
SCORE_LEN = 16


NEGATIVE = -1e30
EPSILON = 1e-05


def alibi_slopes(head_count):
    return jnp.exp2(-8.0 * jnp.arange(1, head_count + 1).astype(jnp.float32) / head_count)


def lse_combine(peak, total, chosen, axis):
    top = jnp.max(peak, axis=axis, keepdims=True)
    total = jnp.sum(total * jnp.exp(peak - top), axis=axis)
    return jnp.squeeze(top, axis), total, jnp.sum(chosen, axis=axis)


def per_device(
    query,
    self_kv,
    kv_pages,
    page_dest,
    page_request,
    score_len,
    out_proj,
    residual,
    norm_gain,
    norm_bias,
    vocab,
    targets,
):
    groups = lax.axis_size("group")
    shards = lax.axis_size("tensor")
    group_id = lax.axis_index("group")
    tensor_id = lax.axis_index("tensor")
    tok_grp = query.shape[1]
    flat_width = query.shape[2]
    head_local = flat_width // HEAD_DIM
    per_owner = kv_pages.shape[1]
    page_len = kv_pages.shape[2]
    capacity = 2 * per_owner // groups
    destination = page_dest[:, 0]
    page_total = destination.shape[0]
    buffer = groups * capacity
    width = residual.shape[2]

    local = jnp.arange(per_owner, dtype=jnp.int32)
    earlier = local[None, :] < local[:, None]
    my_dest = lax.dynamic_slice_in_dim(destination, group_id * per_owner, per_owner)
    my_position = jnp.sum(
        ((my_dest[None, :] == my_dest[:, None]) & earlier).astype(jnp.int32), axis=1
    )
    out_slot = my_dest * capacity + my_position
    slots = jnp.arange(buffer, dtype=jnp.int32)
    send_hot = (out_slot[None, :] == slots[:, None]).astype(kv_pages.dtype)
    outgoing = jnp.einsum(
        "sp,mpjcx->scmjx", send_hot, kv_pages, preferred_element_type=jnp.float32
    ).astype(kv_pages.dtype)
    incoming = lax.all_to_all(
        outgoing.reshape(buffer, -1, flat_width), "group", split_axis=0, concat_axis=0, tiled=True
    ).reshape(outgoing.shape)

    pages = jnp.arange(page_total, dtype=jnp.int32)
    mine = destination == group_id
    mine_blocks = mine.reshape(groups, per_owner)
    rank_in_block = jnp.sum(
        (mine_blocks[:, None, :] & earlier[None]).astype(jnp.int32), axis=2
    ).reshape(-1)
    arrival = (pages // per_owner) * capacity + rank_in_block
    recv_hot = mine[None, :] & (arrival[None, :] == slots[:, None])
    is_valid = jnp.any(recv_hot, axis=1)
    slot_page = jnp.sum(jnp.where(recv_hot, pages[None, :], 0), axis=1)
    slot_request = jnp.sum(jnp.where(recv_hot, page_request[None, :], 0), axis=1)
    slot_rank = jnp.sum(
        (
            mine[None, :]
            & (page_request[None, :] == slot_request[:, None])
            & (pages[None, :] < slot_page[:, None])
        ).astype(jnp.int32),
        axis=1,
    )
    request_ids = jnp.arange(REQ_GRP, dtype=jnp.int32)
    totals = jnp.sum(
        (mine[None, :] & (page_request[None, :] == request_ids[:, None])).astype(jnp.int32),
        axis=1,
    )

    slopes = lax.dynamic_slice_in_dim(alibi_slopes(HEADS), tensor_id * head_local, head_local)
    score_scale = 1.0 / math.sqrt(HEAD_DIM)
    token_ids = jnp.arange(tok_grp, dtype=jnp.int32)
    token_request = token_ids // SCORE_LEN
    token_step = token_ids % SCORE_LEN
    own_distance = (token_step[:, None] - token_step[None, :]).astype(jnp.float32)
    own_allowed = (
        (token_request[:, None] == token_request[None, :])
        & (token_step[None, :] <= token_step[:, None])
    )[None]
    key_request = jnp.repeat(jnp.where(is_valid, slot_request, -1), page_len)
    key_position = (
        slot_rank[:, None] * page_len + jnp.arange(page_len, dtype=jnp.int32)[None, :]
    ).reshape(-1)
    context = totals[token_request] * page_len
    distance = ((context + token_step)[:, None] - key_position[None, :]).astype(jnp.float32)
    allowed = (key_request[None, :] == token_request[:, None])[None]
    page_keys = incoming[:, 0]
    page_values = incoming[:, 1]
    heads_out = []
    for h in range(head_local):
        lanes_h = slice(h * HEAD_DIM, (h + 1) * HEAD_DIM)
        q = query[:, :, lanes_h]
        own_k = self_kv[:, :, 0, lanes_h]
        own_v = self_kv[:, :, 1, lanes_h]
        slope = slopes[h]
        own_scores = (
            jnp.einsum("mtd,msd->mts", q, own_k, preferred_element_type=jnp.float32) * score_scale
        )
        own_scores = own_scores - slope * own_distance[None]
        own_scores = jnp.where(own_allowed, own_scores, NEGATIVE)
        scores = (
            jnp.einsum("mtd,smjd->mtsj", q, page_keys[..., lanes_h],
                       preferred_element_type=jnp.float32).reshape(2, tok_grp, -1) * score_scale
        )
        scores = scores - slope * distance[None]
        scores = jnp.where(allowed, scores, NEGATIVE)
        row_top = jnp.maximum(jnp.max(scores, -1), jnp.max(own_scores, -1))
        exp_terms = jnp.where(allowed, jnp.exp(scores - row_top[..., None]), 0.0)
        own_terms = jnp.where(own_allowed, jnp.exp(own_scores - row_top[..., None]), 0.0)
        denominator = jnp.sum(exp_terms, -1) + jnp.sum(own_terms, -1)
        numerator = jnp.einsum(
            "mtsj,smjd->mtd",
            exp_terms.astype(jnp.bfloat16).reshape(2, tok_grp, buffer, page_len),
            page_values[..., lanes_h],
            preferred_element_type=jnp.float32,
        ) + jnp.einsum(
            "mts,msd->mtd", own_terms.astype(jnp.bfloat16), own_v,
            preferred_element_type=jnp.float32,
        )
        heads_out.append(numerator / denominator[..., None])
    attended = jnp.concatenate(heads_out, axis=-1).astype(jnp.bfloat16)

    rows_local = tok_grp // shards
    partial = jnp.einsum("mtk,mkd->tmd", attended, out_proj, preferred_element_type=jnp.float32)
    parts = lax.all_to_all(
        partial.reshape(shards, rows_local, 2, width), "tensor", 0, 0, tiled=True
    )
    mixed = jnp.sum(parts, axis=0)
    hidden = residual.astype(jnp.float32) + jnp.transpose(mixed, (1, 0, 2))
    row_mean = jnp.mean(hidden, axis=-1, keepdims=True)
    centered = hidden - row_mean
    variance = jnp.mean(centered * centered, axis=-1, keepdims=True)
    normed = (
        centered / jnp.sqrt(variance + EPSILON) * norm_gain[:, None, :] + norm_bias[:, None, :]
    ).astype(jnp.bfloat16)

    voc_local = vocab.shape[2]
    offset = (group_id * shards + tensor_id) * voc_local
    side = tensor_id % 2
    x_size = shards // 2
    x_id = tensor_id // 2
    y_size = 4
    z_size = groups // y_size
    z_id = group_id // y_size
    y_id = group_id % y_size
    swap = [(t, t ^ 1) for t in range(shards)]
    kept = lax.dynamic_index_in_dim(normed, side, 0, keepdims=False)
    given = lax.ppermute(lax.dynamic_index_in_dim(normed, 1 - side, 0, keepdims=False), "tensor", swap)
    block = jnp.where(
        side == 0, jnp.concatenate([kept, given], 0), jnp.concatenate([given, kept], 0)
    )

    def x_shift(step):
        return [(t, (t + 2 * step) % shards) for t in range(shards)]

    def y_shift(step):
        return [(z * y_size + y, z * y_size + (y + step) % y_size)
                for z in range(z_size) for y in range(y_size)]

    def z_shift(step):
        return [(z * y_size + y, ((z + step) % z_size) * y_size + y)
                for z in range(z_size) for y in range(y_size)]

    block = jnp.concatenate(
        [block] + [lax.ppermute(block, "tensor", x_shift(k)) for k in range(1, x_size)], 0
    )
    block = jnp.concatenate(
        [block] + [lax.ppermute(block, "group", y_shift(k)) for k in range(1, y_size)], 0
    )
    forward, backward = block, block
    chunks = [block]
    z_from = [0]
    for k in range(1, z_size // 2 + 1):
        forward = lax.ppermute(forward, "group", z_shift(1))
        chunks.append(forward)
        z_from.append(k)
        if k < z_size // 2:
            backward = lax.ppermute(backward, "group", z_shift(z_size - 1))
            chunks.append(backward)
            z_from.append(z_size - k)
    own_model = jnp.concatenate(chunks, 0)
    other_model = lax.ppermute(own_model, "tensor", swap)
    z_from = jnp.array(z_from, dtype=jnp.int32)
    y_from = jnp.arange(y_size, dtype=jnp.int32)
    source_group = (
        ((z_id - z_from[:, None]) % z_size) * y_size + (y_id - y_from[None, :]) % y_size
    ).reshape(-1)
    x_from = (x_id - jnp.arange(x_size, dtype=jnp.int32)) % x_size
    pair_rows = 2 * rows_local
    wanted = (
        targets.reshape(groups, x_size, pair_rows)[source_group[:, None], x_from[None, :]] - offset
    ).reshape(-1)
    lanes = jnp.arange(voc_local, dtype=jnp.int32)

    def local_stats(rows, weights):
        logits = jnp.dot(rows, weights, preferred_element_type=jnp.float32)
        peak = jnp.max(logits, axis=1)
        total = jnp.sum(jnp.exp(logits - peak[:, None]), axis=1)
        chosen = jnp.sum(jnp.where(lanes[None, :] == wanted[:, None], logits, 0.0), axis=1)
        return jnp.stack([peak, total, chosen])

    own_stats = local_stats(own_model, lax.dynamic_index_in_dim(vocab, side, 0, keepdims=False))
    other_stats = local_stats(
        other_model, lax.dynamic_index_in_dim(vocab, 1 - side, 0, keepdims=False)
    )
    stats = jnp.where(
        side == 0, jnp.stack([own_stats, other_stats], 1), jnp.stack([other_stats, own_stats], 1)
    ).reshape(3, 2, groups, x_size, pair_rows)
    group_at = jnp.zeros((groups,), jnp.int32).at[source_group].set(
        jnp.arange(groups, dtype=jnp.int32)
    )
    x_at = (x_id - jnp.arange(x_size, dtype=jnp.int32)) % x_size
    stats = jnp.take(jnp.take(stats, group_at, axis=2), x_at, axis=3)
    stats = stats.reshape(3, 2, groups, shards, rows_local)

    stats = lax.all_to_all(stats, "tensor", 3, 3, tiled=True)
    peak, total, chosen = lse_combine(stats[0], stats[1], stats[2], 2)
    stats = lax.all_to_all(jnp.stack([peak, total, chosen]), "group", 2, 2, tiled=True)
    peak, total, chosen = lse_combine(stats[0], stats[1], stats[2], 1)
    mine_lp = chosen - (peak + jnp.log(total))

    local_ids = tensor_id * rows_local + jnp.arange(rows_local, dtype=jnp.int32)
    keep_token = local_ids % SCORE_LEN < score_len[local_ids // SCORE_LEN]
    return jnp.where(keep_token[None, :], mine_lp, 0.0)


def solution(mesh):
    in_specs = (
        P(None, "group", "tensor"),
        P(None, "group", None, "tensor"),
        P(None, "group", None, None, "tensor"),
        P(),
        P(),
        P("group"),
        P(None, "tensor", None),
        P(None, ("group", "tensor"), None),
        P(),
        P(),
        P(None, None, ("group", "tensor")),
        P(),
    )
    out_specs = P(None, ("group", "tensor"))
    return jax.shard_map(
        per_device, mesh=mesh, in_specs=in_specs, out_specs=out_specs, check_vma=False
    )
```

```python
import math

import jax
import jax.numpy as jnp
from jax import lax
from jax.sharding import PartitionSpec as P

HEADS = 16
HEAD_DIM = 128
REQ_GRP = 2
SCORE_LEN = 16


NEGATIVE = -1e30
EPSILON = 1e-05


def alibi_slopes(head_count):
    return jnp.exp2(-8.0 * jnp.arange(1, head_count + 1).astype(jnp.float32) / head_count)


def lse_combine(peak, total, chosen, axis):
    top = jnp.max(peak, axis=axis, keepdims=True)
    total = jnp.sum(total * jnp.exp(peak - top), axis=axis)
    return jnp.squeeze(top, axis), total, jnp.sum(chosen, axis=axis)


def per_device(
    query,
    self_kv,
    kv_pages,
    page_dest,
    page_request,
    score_len,
    out_proj,
    residual,
    norm_gain,
    norm_bias,
    vocab,
    targets,
):
    groups = lax.axis_size("group")
    shards = lax.axis_size("tensor")
    group_id = lax.axis_index("group")
    tensor_id = lax.axis_index("tensor")
    tok_grp = query.shape[1]
    flat_width = query.shape[2]
    head_local = flat_width // HEAD_DIM
    per_owner = kv_pages.shape[1]
    page_len = kv_pages.shape[2]
    capacity = 2 * per_owner // groups
    destination = page_dest[:, 0]
    page_total = destination.shape[0]
    buffer = groups * capacity
    width = residual.shape[2]

    local = jnp.arange(per_owner, dtype=jnp.int32)
    earlier = local[None, :] < local[:, None]
    my_dest = lax.dynamic_slice_in_dim(destination, group_id * per_owner, per_owner)
    my_position = jnp.sum(
        ((my_dest[None, :] == my_dest[:, None]) & earlier).astype(jnp.int32), axis=1
    )
    out_slot = my_dest * capacity + my_position
    slots = jnp.arange(buffer, dtype=jnp.int32)
    send_hot = (out_slot[None, :] == slots[:, None]).astype(kv_pages.dtype)
    outgoing = jnp.einsum(
        "sp,mpjcx->scmjx", send_hot, kv_pages, preferred_element_type=jnp.float32
    ).astype(kv_pages.dtype)
    incoming = lax.all_to_all(
        outgoing.reshape(buffer, -1, flat_width), "group", split_axis=0, concat_axis=0, tiled=True
    ).reshape(outgoing.shape)

    pages = jnp.arange(page_total, dtype=jnp.int32)
    mine = destination == group_id
    mine_blocks = mine.reshape(groups, per_owner)
    rank_in_block = jnp.sum(
        (mine_blocks[:, None, :] & earlier[None]).astype(jnp.int32), axis=2
    ).reshape(-1)
    arrival = (pages // per_owner) * capacity + rank_in_block
    recv_hot = mine[None, :] & (arrival[None, :] == slots[:, None])
    is_valid = jnp.any(recv_hot, axis=1)
    slot_page = jnp.sum(jnp.where(recv_hot, pages[None, :], 0), axis=1)
    slot_request = jnp.sum(jnp.where(recv_hot, page_request[None, :], 0), axis=1)
    slot_rank = jnp.sum(
        (
            mine[None, :]
            & (page_request[None, :] == slot_request[:, None])
            & (pages[None, :] < slot_page[:, None])
        ).astype(jnp.int32),
        axis=1,
    )
    request_ids = jnp.arange(REQ_GRP, dtype=jnp.int32)
    totals = jnp.sum(
        (mine[None, :] & (page_request[None, :] == request_ids[:, None])).astype(jnp.int32),
        axis=1,
    )

    slopes = lax.dynamic_slice_in_dim(alibi_slopes(HEADS), tensor_id * head_local, head_local)
    score_scale = 1.0 / math.sqrt(HEAD_DIM)
    token_ids = jnp.arange(tok_grp, dtype=jnp.int32)
    token_request = token_ids // SCORE_LEN
    token_step = token_ids % SCORE_LEN
    own_distance = (token_step[:, None] - token_step[None, :]).astype(jnp.float32)
    own_allowed = (
        (token_request[:, None] == token_request[None, :])
        & (token_step[None, :] <= token_step[:, None])
    )[None]
    key_request = jnp.repeat(jnp.where(is_valid, slot_request, -1), page_len)
    key_position = (
        slot_rank[:, None] * page_len + jnp.arange(page_len, dtype=jnp.int32)[None, :]
    ).reshape(-1)
    context = totals[token_request] * page_len
    distance = ((context + token_step)[:, None] - key_position[None, :]).astype(jnp.float32)
    allowed = (key_request[None, :] == token_request[:, None])[None]
    page_keys = incoming[:, 0]
    page_values = incoming[:, 1]
    heads_out = []
    for h in range(head_local):
        lanes_h = slice(h * HEAD_DIM, (h + 1) * HEAD_DIM)
        q = query[:, :, lanes_h]
        own_k = self_kv[:, :, 0, lanes_h]
        own_v = self_kv[:, :, 1, lanes_h]
        slope = slopes[h]
        own_scores = (
            jnp.einsum("mtd,msd->mts", q, own_k, preferred_element_type=jnp.float32) * score_scale
        )
        own_scores = own_scores - slope * own_distance[None]
        own_scores = jnp.where(own_allowed, own_scores, NEGATIVE)
        scores = (
            jnp.einsum("mtd,smjd->mtsj", q, page_keys[..., lanes_h],
                       preferred_element_type=jnp.float32).reshape(2, tok_grp, -1) * score_scale
        )
        scores = scores - slope * distance[None]
        scores = jnp.where(allowed, scores, NEGATIVE)
        row_top = jnp.maximum(jnp.max(scores, -1), jnp.max(own_scores, -1))
        exp_terms = jnp.where(allowed, jnp.exp(scores - row_top[..., None]), 0.0)
        own_terms = jnp.where(own_allowed, jnp.exp(own_scores - row_top[..., None]), 0.0)
        denominator = jnp.sum(exp_terms, -1) + jnp.sum(own_terms, -1)
        numerator = jnp.einsum(
            "mtsj,smjd->mtd",
            exp_terms.astype(jnp.bfloat16).reshape(2, tok_grp, buffer, page_len),
            page_values[..., lanes_h],
            preferred_element_type=jnp.float32,
        ) + jnp.einsum(
            "mts,msd->mtd", own_terms.astype(jnp.bfloat16), own_v,
            preferred_element_type=jnp.float32,
        )
        heads_out.append(numerator / denominator[..., None])
    attended = jnp.concatenate(heads_out, axis=-1).astype(jnp.bfloat16)

    rows_local = tok_grp // shards
    partial = jnp.einsum("mtk,mkd->tmd", attended, out_proj, preferred_element_type=jnp.float32)
    parts = lax.all_to_all(
        partial.reshape(shards, rows_local, 2, width), "tensor", 0, 0, tiled=True
    )
    mixed = jnp.sum(parts, axis=0)
    hidden = residual.astype(jnp.float32) + jnp.transpose(mixed, (1, 0, 2))
    row_mean = jnp.mean(hidden, axis=-1, keepdims=True)
    centered = hidden - row_mean
    variance = jnp.mean(centered * centered, axis=-1, keepdims=True)
    normed = (
        centered / jnp.sqrt(variance + EPSILON) * norm_gain[:, None, :] + norm_bias[:, None, :]
    ).astype(jnp.bfloat16)

    voc_local = vocab.shape[2]
    offset = (group_id * shards + tensor_id) * voc_local
    side = tensor_id % 2
    x_size = shards // 2
    x_id = tensor_id // 2
    y_size = 4
    z_size = groups // y_size
    z_id = group_id // y_size
    y_id = group_id % y_size
    swap = [(t, t ^ 1) for t in range(shards)]
    kept = lax.dynamic_index_in_dim(normed, side, 0, keepdims=False)
    given = lax.ppermute(lax.dynamic_index_in_dim(normed, 1 - side, 0, keepdims=False), "tensor", swap)
    block = jnp.where(
        side == 0, jnp.concatenate([kept, given], 0), jnp.concatenate([given, kept], 0)
    )

    def x_shift(step):
        return [(t, (t + 2 * step) % shards) for t in range(shards)]

    def y_shift(step):
        return [(z * y_size + y, z * y_size + (y + step) % y_size)
                for z in range(z_size) for y in range(y_size)]

    def z_shift(step):
        return [(z * y_size + y, ((z + step) % z_size) * y_size + y)
                for z in range(z_size) for y in range(y_size)]

    block = jnp.concatenate(
        [block] + [lax.ppermute(block, "tensor", x_shift(k)) for k in range(1, x_size)], 0
    )
    block = jnp.concatenate(
        [block] + [lax.ppermute(block, "group", y_shift(k)) for k in range(1, y_size)], 0
    )
    forward, backward = block, block
    chunks = [block]
    z_from = [0]
    for k in range(1, z_size // 2 + 1):
        forward = lax.ppermute(forward, "group", z_shift(1))
        chunks.append(forward)
        z_from.append(k)
        if k < z_size // 2:
            backward = lax.ppermute(backward, "group", z_shift(z_size - 1))
            chunks.append(backward)
            z_from.append(z_size - k)
    z_from = jnp.array(z_from, dtype=jnp.int32)
    y_from = jnp.arange(y_size, dtype=jnp.int32)
    source_group = (
        ((z_id - z_from[:, None]) % z_size) * y_size + (y_id - y_from[None, :]) % y_size
    ).reshape(-1)
    x_from = (x_id - jnp.arange(x_size, dtype=jnp.int32)) % x_size
    pair_rows = 2 * rows_local
    wanted = (
        targets.reshape(groups, x_size, pair_rows)[source_group[:, None], x_from[None, :]] - offset
    ).reshape(-1)
    lanes = jnp.arange(voc_local, dtype=jnp.int32)

    def local_stats(rows, weights, wanted_rows):
        logits = jnp.dot(rows, weights, preferred_element_type=jnp.float32)
        peak = jnp.max(logits, axis=1)
        total = jnp.sum(jnp.exp(logits - peak[:, None]), axis=1)
        chosen = jnp.sum(jnp.where(lanes[None, :] == wanted_rows[:, None], logits, 0.0), axis=1)
        return jnp.stack([peak, total, chosen])

    own_weights = lax.dynamic_index_in_dim(vocab, side, 0, keepdims=False)
    other_weights = lax.dynamic_index_in_dim(vocab, 1 - side, 0, keepdims=False)
    chunk_rows = chunks[0].shape[0]
    own_parts, other_parts = [], []
    for i, rows in enumerate(chunks):
        wanted_i = wanted[i * chunk_rows:(i + 1) * chunk_rows]
        own_parts.append(local_stats(rows, own_weights, wanted_i))
        mate_rows = lax.ppermute(rows, "tensor", swap)
        other_parts.append(local_stats(mate_rows, other_weights, wanted_i))
    own_stats = jnp.concatenate(own_parts, 1)
    other_stats = jnp.concatenate(other_parts, 1)
    stats = jnp.where(
        side == 0, jnp.stack([own_stats, other_stats], 1), jnp.stack([other_stats, own_stats], 1)
    ).reshape(3, 2, groups, x_size, pair_rows)
    group_at = jnp.zeros((groups,), jnp.int32).at[source_group].set(
        jnp.arange(groups, dtype=jnp.int32)
    )
    x_at = (x_id - jnp.arange(x_size, dtype=jnp.int32)) % x_size
    stats = jnp.take(jnp.take(stats, group_at, axis=2), x_at, axis=3)
    stats = stats.reshape(3, 2, groups, shards, rows_local)

    stats = lax.all_to_all(stats, "tensor", 3, 3, tiled=True)
    peak, total, chosen = lse_combine(stats[0], stats[1], stats[2], 2)
    stats = lax.all_to_all(jnp.stack([peak, total, chosen]), "group", 2, 2, tiled=True)
    peak, total, chosen = lse_combine(stats[0], stats[1], stats[2], 1)
    mine_lp = chosen - (peak + jnp.log(total))

    local_ids = tensor_id * rows_local + jnp.arange(rows_local, dtype=jnp.int32)
    keep_token = local_ids % SCORE_LEN < score_len[local_ids // SCORE_LEN]
    return jnp.where(keep_token[None, :], mine_lp, 0.0)


def solution(mesh):
    in_specs = (
        P(None, "group", "tensor"),
        P(None, "group", None, "tensor"),
        P(None, "group", None, None, "tensor"),
        P(),
        P(),
        P("group"),
        P(None, "tensor", None),
        P(None, ("group", "tensor"), None),
        P(),
        P(),
        P(None, None, ("group", "tensor")),
        P(),
    )
    out_specs = P(None, ("group", "tensor"))
    return jax.shard_map(
        per_device, mesh=mesh, in_specs=in_specs, out_specs=out_specs, check_vma=False
    )
```

```python
import math

import jax
import jax.numpy as jnp
from jax import lax
from jax.sharding import PartitionSpec as P

HEADS = 16
HEAD_DIM = 128
REQ_GRP = 2
SCORE_LEN = 16


NEGATIVE = -1e30
EPSILON = 1e-05


def alibi_slopes(head_count):
    return jnp.exp2(-8.0 * jnp.arange(1, head_count + 1).astype(jnp.float32) / head_count)


def lse_combine(peak, total, chosen, axis):
    top = jnp.max(peak, axis=axis, keepdims=True)
    total = jnp.sum(total * jnp.exp(peak - top), axis=axis)
    return jnp.squeeze(top, axis), total, jnp.sum(chosen, axis=axis)


def per_device(
    query,
    self_kv,
    kv_pages,
    page_dest,
    page_request,
    score_len,
    out_proj,
    residual,
    norm_gain,
    norm_bias,
    vocab,
    targets,
):
    groups = lax.axis_size("group")
    shards = lax.axis_size("tensor")
    group_id = lax.axis_index("group")
    tensor_id = lax.axis_index("tensor")
    tok_grp = query.shape[1]
    flat_width = query.shape[2]
    head_local = flat_width // HEAD_DIM
    per_owner = kv_pages.shape[1]
    page_len = kv_pages.shape[2]
    capacity = 2 * per_owner // groups
    destination = page_dest[:, 0]
    page_total = destination.shape[0]
    buffer = groups * capacity
    width = residual.shape[2]

    local = jnp.arange(per_owner, dtype=jnp.int32)
    earlier = local[None, :] < local[:, None]
    my_dest = lax.dynamic_slice_in_dim(destination, group_id * per_owner, per_owner)
    my_position = jnp.sum(
        ((my_dest[None, :] == my_dest[:, None]) & earlier).astype(jnp.int32), axis=1
    )
    out_slot = my_dest * capacity + my_position
    slots = jnp.arange(buffer, dtype=jnp.int32)
    send_hot = (out_slot[None, :] == slots[:, None]).astype(kv_pages.dtype)
    outgoing = jnp.einsum(
        "sp,mpjcx->scmjx", send_hot, kv_pages, preferred_element_type=jnp.float32
    ).astype(kv_pages.dtype)
    incoming = lax.all_to_all(
        outgoing.reshape(buffer, -1, flat_width), "group", split_axis=0, concat_axis=0, tiled=True
    ).reshape(outgoing.shape)

    pages = jnp.arange(page_total, dtype=jnp.int32)
    mine = destination == group_id
    mine_blocks = mine.reshape(groups, per_owner)
    rank_in_block = jnp.sum(
        (mine_blocks[:, None, :] & earlier[None]).astype(jnp.int32), axis=2
    ).reshape(-1)
    arrival = (pages // per_owner) * capacity + rank_in_block
    recv_hot = mine[None, :] & (arrival[None, :] == slots[:, None])
    is_valid = jnp.any(recv_hot, axis=1)
    slot_page = jnp.sum(jnp.where(recv_hot, pages[None, :], 0), axis=1)
    slot_request = jnp.sum(jnp.where(recv_hot, page_request[None, :], 0), axis=1)
    slot_rank = jnp.sum(
        (
            mine[None, :]
            & (page_request[None, :] == slot_request[:, None])
            & (pages[None, :] < slot_page[:, None])
        ).astype(jnp.int32),
        axis=1,
    )
    request_ids = jnp.arange(REQ_GRP, dtype=jnp.int32)
    totals = jnp.sum(
        (mine[None, :] & (page_request[None, :] == request_ids[:, None])).astype(jnp.int32),
        axis=1,
    )

    slopes = lax.dynamic_slice_in_dim(alibi_slopes(HEADS), tensor_id * head_local, head_local)
    score_scale = 1.0 / math.sqrt(HEAD_DIM)
    token_ids = jnp.arange(tok_grp, dtype=jnp.int32)
    token_request = token_ids // SCORE_LEN
    token_step = token_ids % SCORE_LEN
    own_distance = (token_step[:, None] - token_step[None, :]).astype(jnp.float32)
    own_allowed = (
        (token_request[:, None] == token_request[None, :])
        & (token_step[None, :] <= token_step[:, None])
    )[None]
    key_request = jnp.repeat(jnp.where(is_valid, slot_request, -1), page_len)
    key_position = (
        slot_rank[:, None] * page_len + jnp.arange(page_len, dtype=jnp.int32)[None, :]
    ).reshape(-1)
    context = totals[token_request] * page_len
    distance = ((context + token_step)[:, None] - key_position[None, :]).astype(jnp.float32)
    allowed = (key_request[None, :] == token_request[:, None])[None]
    page_keys = incoming[:, 0]
    page_values = incoming[:, 1]
    heads_out = []
    for h in range(head_local):
        lanes_h = slice(h * HEAD_DIM, (h + 1) * HEAD_DIM)
        q = query[:, :, lanes_h]
        own_k = self_kv[:, :, 0, lanes_h]
        own_v = self_kv[:, :, 1, lanes_h]
        slope = slopes[h]
        own_scores = (
            jnp.einsum("mtd,msd->mts", q, own_k, preferred_element_type=jnp.float32) * score_scale
        )
        own_scores = own_scores - slope * own_distance[None]
        own_scores = jnp.where(own_allowed, own_scores, NEGATIVE)
        scores = (
            jnp.einsum("mtd,smjd->mtsj", q, page_keys[..., lanes_h],
                       preferred_element_type=jnp.float32).reshape(2, tok_grp, -1) * score_scale
        )
        scores = scores - slope * distance[None]
        scores = jnp.where(allowed, scores, NEGATIVE)
        row_top = jnp.maximum(jnp.max(scores, -1), jnp.max(own_scores, -1))
        exp_terms = jnp.where(allowed, jnp.exp(scores - row_top[..., None]), 0.0)
        own_terms = jnp.where(own_allowed, jnp.exp(own_scores - row_top[..., None]), 0.0)
        denominator = jnp.sum(exp_terms, -1) + jnp.sum(own_terms, -1)
        numerator = jnp.einsum(
            "mtsj,smjd->mtd",
            exp_terms.astype(jnp.bfloat16).reshape(2, tok_grp, buffer, page_len),
            page_values[..., lanes_h],
            preferred_element_type=jnp.float32,
        ) + jnp.einsum(
            "mts,msd->mtd", own_terms.astype(jnp.bfloat16), own_v,
            preferred_element_type=jnp.float32,
        )
        heads_out.append(numerator / denominator[..., None])
    attended = jnp.concatenate(heads_out, axis=-1).astype(jnp.bfloat16)

    rows_local = tok_grp // shards
    partial = jnp.einsum("mtk,mkd->tmd", attended, out_proj, preferred_element_type=jnp.float32)
    parts = lax.all_to_all(
        partial.reshape(shards, rows_local, 2, width), "tensor", 0, 0, tiled=True
    )
    mixed = jnp.sum(parts, axis=0)
    hidden = residual.astype(jnp.float32) + jnp.transpose(mixed, (1, 0, 2))
    row_mean = jnp.mean(hidden, axis=-1, keepdims=True)
    centered = hidden - row_mean
    variance = jnp.mean(centered * centered, axis=-1, keepdims=True)
    normed = (
        centered / jnp.sqrt(variance + EPSILON) * norm_gain[:, None, :] + norm_bias[:, None, :]
    ).astype(jnp.bfloat16)

    voc_local = vocab.shape[2]
    offset = (group_id * shards + tensor_id) * voc_local
    side = tensor_id % 2
    x_size = shards // 2
    x_id = tensor_id // 2
    y_size = 4
    z_size = groups // y_size
    z_id = group_id // y_size
    y_id = group_id % y_size
    swap = [(t, t ^ 1) for t in range(shards)]
    kept = lax.dynamic_index_in_dim(normed, side, 0, keepdims=False)
    given = lax.ppermute(lax.dynamic_index_in_dim(normed, 1 - side, 0, keepdims=False), "tensor", swap)
    block = jnp.where(
        side == 0, jnp.concatenate([kept, given], 0), jnp.concatenate([given, kept], 0)
    )

    def x_shift(step):
        return [(t, (t + 2 * step) % shards) for t in range(shards)]

    def y_shift(step):
        return [(z * y_size + y, z * y_size + (y + step) % y_size)
                for z in range(z_size) for y in range(y_size)]

    def z_shift(step):
        return [(z * y_size + y, ((z + step) % z_size) * y_size + y)
                for z in range(z_size) for y in range(y_size)]

    block = jnp.concatenate(
        [block] + [lax.ppermute(block, "tensor", x_shift(k)) for k in range(1, x_size)], 0
    )
    block = jnp.concatenate(
        [block] + [lax.ppermute(block, "group", y_shift(k)) for k in range(1, y_size)], 0
    )
    forward, backward = block, block
    chunks = [block]
    z_from = [0]
    for k in range(1, z_size // 2):
        forward = lax.ppermute(forward, "group", z_shift(1))
        chunks.append(forward)
        z_from.append(k)
        backward = lax.ppermute(backward, "group", z_shift(z_size - 1))
        chunks.append(backward)
        z_from.append(z_size - k)
    split = block.shape[0] // 2
    chunks.append(jnp.concatenate([
        lax.ppermute(forward[:split], "group", z_shift(1)),
        lax.ppermute(backward[split:], "group", z_shift(z_size - 1)),
    ], 0))
    z_from.append(z_size // 2)
    own_model = jnp.concatenate(chunks, 0)
    other_model = lax.ppermute(own_model, "tensor", swap)
    z_from = jnp.array(z_from, dtype=jnp.int32)
    y_from = jnp.arange(y_size, dtype=jnp.int32)
    source_group = (
        ((z_id - z_from[:, None]) % z_size) * y_size + (y_id - y_from[None, :]) % y_size
    ).reshape(-1)
    x_from = (x_id - jnp.arange(x_size, dtype=jnp.int32)) % x_size
    pair_rows = 2 * rows_local
    wanted = (
        targets.reshape(groups, x_size, pair_rows)[source_group[:, None], x_from[None, :]] - offset
    ).reshape(-1)
    lanes = jnp.arange(voc_local, dtype=jnp.int32)

    def local_stats(rows, weights):
        logits = jnp.dot(rows, weights, preferred_element_type=jnp.float32)
        peak = jnp.max(logits, axis=1)
        total = jnp.sum(jnp.exp(logits - peak[:, None]), axis=1)
        chosen = jnp.sum(jnp.where(lanes[None, :] == wanted[:, None], logits, 0.0), axis=1)
        return jnp.stack([peak, total, chosen])

    own_stats = local_stats(own_model, lax.dynamic_index_in_dim(vocab, side, 0, keepdims=False))
    other_stats = local_stats(
        other_model, lax.dynamic_index_in_dim(vocab, 1 - side, 0, keepdims=False)
    )
    stats = jnp.where(
        side == 0, jnp.stack([own_stats, other_stats], 1), jnp.stack([other_stats, own_stats], 1)
    ).reshape(3, 2, groups, x_size, pair_rows)
    group_at = jnp.zeros((groups,), jnp.int32).at[source_group].set(
        jnp.arange(groups, dtype=jnp.int32)
    )
    x_at = (x_id - jnp.arange(x_size, dtype=jnp.int32)) % x_size
    stats = jnp.take(jnp.take(stats, group_at, axis=2), x_at, axis=3)
    stats = stats.reshape(3, 2, groups, shards, rows_local)

    stats = lax.all_to_all(stats, "tensor", 3, 3, tiled=True)
    peak, total, chosen = lse_combine(stats[0], stats[1], stats[2], 2)
    stats = lax.all_to_all(jnp.stack([peak, total, chosen]), "group", 2, 2, tiled=True)
    peak, total, chosen = lse_combine(stats[0], stats[1], stats[2], 1)
    mine_lp = chosen - (peak + jnp.log(total))

    local_ids = tensor_id * rows_local + jnp.arange(rows_local, dtype=jnp.int32)
    keep_token = local_ids % SCORE_LEN < score_len[local_ids // SCORE_LEN]
    return jnp.where(keep_token[None, :], mine_lp, 0.0)


def solution(mesh):
    in_specs = (
        P(None, "group", "tensor"),
        P(None, "group", None, "tensor"),
        P(None, "group", None, None, "tensor"),
        P(),
        P(),
        P("group"),
        P(None, "tensor", None),
        P(None, ("group", "tensor"), None),
        P(),
        P(),
        P(None, None, ("group", "tensor")),
        P(),
    )
    out_specs = P(None, ("group", "tensor"))
    return jax.shard_map(
        per_device, mesh=mesh, in_specs=in_specs, out_specs=out_specs, check_vma=False
    )
```

```python
import math

import jax
import jax.numpy as jnp
from jax import lax
from jax.sharding import PartitionSpec as P

HEADS = 16
HEAD_DIM = 128
REQ_GRP = 2
SCORE_LEN = 16


NEGATIVE = -1e30
EPSILON = 1e-05


def alibi_slopes(head_count):
    return jnp.exp2(-8.0 * jnp.arange(1, head_count + 1).astype(jnp.float32) / head_count)


def lse_combine(peak, total, chosen, axis):
    top = jnp.max(peak, axis=axis, keepdims=True)
    total = jnp.sum(total * jnp.exp(peak - top), axis=axis)
    return jnp.squeeze(top, axis), total, jnp.sum(chosen, axis=axis)


def per_device(
    query,
    self_kv,
    kv_pages,
    page_dest,
    page_request,
    score_len,
    out_proj,
    residual,
    norm_gain,
    norm_bias,
    vocab,
    targets,
):
    groups = lax.axis_size("group")
    shards = lax.axis_size("tensor")
    group_id = lax.axis_index("group")
    tensor_id = lax.axis_index("tensor")
    tok_grp = query.shape[1]
    flat_width = query.shape[2]
    head_local = flat_width // HEAD_DIM
    per_owner = kv_pages.shape[1]
    page_len = kv_pages.shape[2]
    capacity = 2 * per_owner // groups
    destination = page_dest[:, 0]
    page_total = destination.shape[0]
    buffer = groups * capacity
    width = residual.shape[2]

    local = jnp.arange(per_owner, dtype=jnp.int32)
    earlier = local[None, :] < local[:, None]
    my_dest = lax.dynamic_slice_in_dim(destination, group_id * per_owner, per_owner)
    my_position = jnp.sum(
        ((my_dest[None, :] == my_dest[:, None]) & earlier).astype(jnp.int32), axis=1
    )
    out_slot = my_dest * capacity + my_position
    slots = jnp.arange(buffer, dtype=jnp.int32)
    send_hot = (out_slot[None, :] == slots[:, None]).astype(kv_pages.dtype)
    outgoing = jnp.einsum(
        "sp,mpjcx->scmjx", send_hot, kv_pages, preferred_element_type=jnp.float32
    ).astype(kv_pages.dtype)
    incoming = lax.all_to_all(
        outgoing.reshape(buffer, -1, flat_width), "group", split_axis=0, concat_axis=0, tiled=True
    ).reshape(outgoing.shape)

    pages = jnp.arange(page_total, dtype=jnp.int32)
    mine = destination == group_id
    mine_blocks = mine.reshape(groups, per_owner)
    rank_in_block = jnp.sum(
        (mine_blocks[:, None, :] & earlier[None]).astype(jnp.int32), axis=2
    ).reshape(-1)
    arrival = (pages // per_owner) * capacity + rank_in_block
    recv_hot = mine[None, :] & (arrival[None, :] == slots[:, None])
    is_valid = jnp.any(recv_hot, axis=1)
    slot_page = jnp.sum(jnp.where(recv_hot, pages[None, :], 0), axis=1)
    slot_request = jnp.sum(jnp.where(recv_hot, page_request[None, :], 0), axis=1)
    slot_rank = jnp.sum(
        (
            mine[None, :]
            & (page_request[None, :] == slot_request[:, None])
            & (pages[None, :] < slot_page[:, None])
        ).astype(jnp.int32),
        axis=1,
    )
    request_ids = jnp.arange(REQ_GRP, dtype=jnp.int32)
    totals = jnp.sum(
        (mine[None, :] & (page_request[None, :] == request_ids[:, None])).astype(jnp.int32),
        axis=1,
    )

    slopes = lax.dynamic_slice_in_dim(alibi_slopes(HEADS), tensor_id * head_local, head_local)
    score_scale = 1.0 / math.sqrt(HEAD_DIM)
    token_ids = jnp.arange(tok_grp, dtype=jnp.int32)
    token_request = token_ids // SCORE_LEN
    token_step = token_ids % SCORE_LEN
    own_distance = (token_step[:, None] - token_step[None, :]).astype(jnp.float32)
    own_allowed = (
        (token_request[:, None] == token_request[None, :])
        & (token_step[None, :] <= token_step[:, None])
    )[None]
    key_request = jnp.repeat(jnp.where(is_valid, slot_request, -1), page_len)
    key_position = (
        slot_rank[:, None] * page_len + jnp.arange(page_len, dtype=jnp.int32)[None, :]
    ).reshape(-1)
    context = totals[token_request] * page_len
    distance = ((context + token_step)[:, None] - key_position[None, :]).astype(jnp.float32)
    allowed = (key_request[None, :] == token_request[:, None])[None]
    page_keys = incoming[:, 0]
    page_values = incoming[:, 1]
    heads_out = []
    for h in range(head_local):
        lanes_h = slice(h * HEAD_DIM, (h + 1) * HEAD_DIM)
        q = query[:, :, lanes_h]
        own_k = self_kv[:, :, 0, lanes_h]
        own_v = self_kv[:, :, 1, lanes_h]
        slope = slopes[h]
        own_scores = (
            jnp.einsum("mtd,msd->mts", q, own_k, preferred_element_type=jnp.float32) * score_scale
        )
        own_scores = own_scores - slope * own_distance[None]
        own_scores = jnp.where(own_allowed, own_scores, NEGATIVE)
        scores = (
            jnp.einsum("mtd,smjd->mtsj", q, page_keys[..., lanes_h],
                       preferred_element_type=jnp.float32).reshape(2, tok_grp, -1) * score_scale
        )
        scores = scores - slope * distance[None]
        scores = jnp.where(allowed, scores, NEGATIVE)
        row_top = jnp.maximum(jnp.max(scores, -1), jnp.max(own_scores, -1))
        exp_terms = jnp.where(allowed, jnp.exp(scores - row_top[..., None]), 0.0)
        own_terms = jnp.where(own_allowed, jnp.exp(own_scores - row_top[..., None]), 0.0)
        denominator = jnp.sum(exp_terms, -1) + jnp.sum(own_terms, -1)
        numerator = jnp.einsum(
            "mtsj,smjd->mtd",
            exp_terms.astype(jnp.bfloat16).reshape(2, tok_grp, buffer, page_len),
            page_values[..., lanes_h],
            preferred_element_type=jnp.float32,
        ) + jnp.einsum(
            "mts,msd->mtd", own_terms.astype(jnp.bfloat16), own_v,
            preferred_element_type=jnp.float32,
        )
        heads_out.append(numerator / denominator[..., None])
    attended = jnp.concatenate(heads_out, axis=-1).astype(jnp.bfloat16)

    rows_local = tok_grp // shards
    side = tensor_id % 2
    x_size = shards // 2
    x_id = tensor_id // 2
    swap = [(t, t ^ 1) for t in range(shards)]

    def x_shift(step):
        return [(t, (t + 2 * step) % shards) for t in range(shards)]

    partial = jnp.einsum("mtk,mkd->tmd", attended, out_proj, preferred_element_type=jnp.float32)
    partial = partial.reshape(x_size, 2, rows_local, 2, width)
    pair_sum = lax.dynamic_index_in_dim(partial, side, 1, keepdims=False) + lax.ppermute(
        lax.dynamic_index_in_dim(partial, 1 - side, 1, keepdims=False), "tensor", swap
    )
    mixed = lax.dynamic_index_in_dim(pair_sum, x_id, 0, keepdims=False)
    for k in range(1, x_size):
        mixed = mixed + lax.ppermute(
            lax.dynamic_index_in_dim(pair_sum, (x_id + k) % x_size, 0, keepdims=False),
            "tensor", x_shift(k),
        )
    hidden = residual.astype(jnp.float32) + jnp.transpose(mixed, (1, 0, 2))
    row_mean = jnp.mean(hidden, axis=-1, keepdims=True)
    centered = hidden - row_mean
    variance = jnp.mean(centered * centered, axis=-1, keepdims=True)
    normed = (
        centered / jnp.sqrt(variance + EPSILON) * norm_gain[:, None, :] + norm_bias[:, None, :]
    ).astype(jnp.bfloat16)

    voc_local = vocab.shape[2]
    offset = (group_id * shards + tensor_id) * voc_local
    y_size = 4
    z_size = groups // y_size
    z_id = group_id // y_size
    y_id = group_id % y_size
    kept = lax.dynamic_index_in_dim(normed, side, 0, keepdims=False)
    given = lax.ppermute(lax.dynamic_index_in_dim(normed, 1 - side, 0, keepdims=False), "tensor", swap)
    block = jnp.where(
        side == 0, jnp.concatenate([kept, given], 0), jnp.concatenate([given, kept], 0)
    )

    def y_shift(step):
        return [(z * y_size + y, z * y_size + (y + step) % y_size)
                for z in range(z_size) for y in range(y_size)]

    def z_shift(step):
        return [(z * y_size + y, ((z + step) % z_size) * y_size + y)
                for z in range(z_size) for y in range(y_size)]

    block = jnp.concatenate(
        [block] + [lax.ppermute(block, "tensor", x_shift(k)) for k in range(1, x_size)], 0
    )
    block = jnp.concatenate(
        [block] + [lax.ppermute(block, "group", y_shift(k)) for k in range(1, y_size)], 0
    )
    forward, backward = block, block
    chunks = [block]
    z_from = [0]
    for k in range(1, z_size // 2):
        forward = lax.ppermute(forward, "group", z_shift(1))
        chunks.append(forward)
        z_from.append(k)
        backward = lax.ppermute(backward, "group", z_shift(z_size - 1))
        chunks.append(backward)
        z_from.append(z_size - k)
    split = block.shape[0] // 2
    chunks.append(jnp.concatenate([
        lax.ppermute(forward[:split], "group", z_shift(1)),
        lax.ppermute(backward[split:], "group", z_shift(z_size - 1)),
    ], 0))
    z_from.append(z_size // 2)
    own_model = jnp.concatenate(chunks, 0)
    other_model = lax.ppermute(own_model, "tensor", swap)
    z_from = jnp.array(z_from, dtype=jnp.int32)
    y_from = jnp.arange(y_size, dtype=jnp.int32)
    source_group = (
        ((z_id - z_from[:, None]) % z_size) * y_size + (y_id - y_from[None, :]) % y_size
    ).reshape(-1)
    x_from = (x_id - jnp.arange(x_size, dtype=jnp.int32)) % x_size
    pair_rows = 2 * rows_local
    wanted = (
        targets.reshape(groups, x_size, pair_rows)[source_group[:, None], x_from[None, :]] - offset
    ).reshape(-1)
    lanes = jnp.arange(voc_local, dtype=jnp.int32)

    def local_stats(rows, weights):
        logits = jnp.dot(rows, weights, preferred_element_type=jnp.float32)
        peak = jnp.max(logits, axis=1)
        total = jnp.sum(jnp.exp(logits - peak[:, None]), axis=1)
        chosen = jnp.sum(jnp.where(lanes[None, :] == wanted[:, None], logits, 0.0), axis=1)
        return jnp.stack([peak, total, chosen])

    own_stats = local_stats(own_model, lax.dynamic_index_in_dim(vocab, side, 0, keepdims=False))
    other_stats = local_stats(
        other_model, lax.dynamic_index_in_dim(vocab, 1 - side, 0, keepdims=False)
    )
    stats = jnp.where(
        side == 0, jnp.stack([own_stats, other_stats], 1), jnp.stack([other_stats, own_stats], 1)
    ).reshape(3, 2, groups, x_size, pair_rows)
    group_at = jnp.zeros((groups,), jnp.int32).at[source_group].set(
        jnp.arange(groups, dtype=jnp.int32)
    )
    x_at = (x_id - jnp.arange(x_size, dtype=jnp.int32)) % x_size
    stats = jnp.take(jnp.take(stats, group_at, axis=2), x_at, axis=3)
    stats = stats.reshape(3, 2, groups, shards, rows_local)

    stats = lax.all_to_all(stats, "tensor", 3, 3, tiled=True)
    peak, total, chosen = lse_combine(stats[0], stats[1], stats[2], 2)
    stats = lax.all_to_all(jnp.stack([peak, total, chosen]), "group", 2, 2, tiled=True)
    peak, total, chosen = lse_combine(stats[0], stats[1], stats[2], 1)
    mine_lp = chosen - (peak + jnp.log(total))

    local_ids = tensor_id * rows_local + jnp.arange(rows_local, dtype=jnp.int32)
    keep_token = local_ids % SCORE_LEN < score_len[local_ids // SCORE_LEN]
    return jnp.where(keep_token[None, :], mine_lp, 0.0)


def solution(mesh):
    in_specs = (
        P(None, "group", "tensor"),
        P(None, "group", None, "tensor"),
        P(None, "group", None, None, "tensor"),
        P(),
        P(),
        P("group"),
        P(None, "tensor", None),
        P(None, ("group", "tensor"), None),
        P(),
        P(),
        P(None, None, ("group", "tensor")),
        P(),
    )
    out_specs = P(None, ("group", "tensor"))
    return jax.shard_map(
        per_device, mesh=mesh, in_specs=in_specs, out_specs=out_specs, check_vma=False
    )
```

```python
import math

import jax
import jax.numpy as jnp
from jax import lax
from jax.sharding import PartitionSpec as P

HEADS = 16
HEAD_DIM = 128
REQ_GRP = 2
SCORE_LEN = 16


NEGATIVE = -1e30
EPSILON = 1e-05


def alibi_slopes(head_count):
    return jnp.exp2(-8.0 * jnp.arange(1, head_count + 1).astype(jnp.float32) / head_count)


def lse_combine(peak, total, chosen, axis):
    top = jnp.max(peak, axis=axis, keepdims=True)
    total = jnp.sum(total * jnp.exp(peak - top), axis=axis)
    return jnp.squeeze(top, axis), total, jnp.sum(chosen, axis=axis)


def per_device(
    query,
    self_kv,
    kv_pages,
    page_dest,
    page_request,
    score_len,
    out_proj,
    residual,
    norm_gain,
    norm_bias,
    vocab,
    targets,
):
    groups = lax.axis_size("group")
    shards = lax.axis_size("tensor")
    group_id = lax.axis_index("group")
    tensor_id = lax.axis_index("tensor")
    tok_grp = query.shape[1]
    flat_width = query.shape[2]
    head_local = flat_width // HEAD_DIM
    per_owner = kv_pages.shape[1]
    page_len = kv_pages.shape[2]
    capacity = 2 * per_owner // groups
    destination = page_dest[:, 0]
    page_total = destination.shape[0]
    buffer = groups * capacity
    width = residual.shape[2]

    local = jnp.arange(per_owner, dtype=jnp.int32)
    earlier = local[None, :] < local[:, None]
    my_dest = lax.dynamic_slice_in_dim(destination, group_id * per_owner, per_owner)
    my_position = jnp.sum(
        ((my_dest[None, :] == my_dest[:, None]) & earlier).astype(jnp.int32), axis=1
    )
    out_slot = my_dest * capacity + my_position
    slots = jnp.arange(buffer, dtype=jnp.int32)
    send_hot = (out_slot[None, :] == slots[:, None]).astype(kv_pages.dtype)
    outgoing = jnp.einsum(
        "sp,mpjcx->scmjx", send_hot, kv_pages, preferred_element_type=jnp.float32
    ).astype(kv_pages.dtype)
    incoming = lax.all_to_all(
        outgoing.reshape(buffer, -1, flat_width), "group", split_axis=0, concat_axis=0, tiled=True
    ).reshape(outgoing.shape)

    pages = jnp.arange(page_total, dtype=jnp.int32)
    mine = destination == group_id
    mine_blocks = mine.reshape(groups, per_owner)
    rank_in_block = jnp.sum(
        (mine_blocks[:, None, :] & earlier[None]).astype(jnp.int32), axis=2
    ).reshape(-1)
    arrival = (pages // per_owner) * capacity + rank_in_block
    recv_hot = mine[None, :] & (arrival[None, :] == slots[:, None])
    is_valid = jnp.any(recv_hot, axis=1)
    slot_page = jnp.sum(jnp.where(recv_hot, pages[None, :], 0), axis=1)
    slot_request = jnp.sum(jnp.where(recv_hot, page_request[None, :], 0), axis=1)
    slot_rank = jnp.sum(
        (
            mine[None, :]
            & (page_request[None, :] == slot_request[:, None])
            & (pages[None, :] < slot_page[:, None])
        ).astype(jnp.int32),
        axis=1,
    )
    request_ids = jnp.arange(REQ_GRP, dtype=jnp.int32)
    totals = jnp.sum(
        (mine[None, :] & (page_request[None, :] == request_ids[:, None])).astype(jnp.int32),
        axis=1,
    )

    slopes = lax.dynamic_slice_in_dim(alibi_slopes(HEADS), tensor_id * head_local, head_local)
    score_scale = 1.0 / math.sqrt(HEAD_DIM)
    token_ids = jnp.arange(tok_grp, dtype=jnp.int32)
    token_request = token_ids // SCORE_LEN
    token_step = token_ids % SCORE_LEN
    own_distance = (token_step[:, None] - token_step[None, :]).astype(jnp.float32)
    own_allowed = (
        (token_request[:, None] == token_request[None, :])
        & (token_step[None, :] <= token_step[:, None])
    )[None]
    key_request = jnp.repeat(jnp.where(is_valid, slot_request, -1), page_len)
    key_position = (
        slot_rank[:, None] * page_len + jnp.arange(page_len, dtype=jnp.int32)[None, :]
    ).reshape(-1)
    context = totals[token_request] * page_len
    distance = ((context + token_step)[:, None] - key_position[None, :]).astype(jnp.float32)
    allowed = (key_request[None, :] == token_request[:, None])[None]
    page_keys = incoming[:, 0]
    page_values = incoming[:, 1]
    heads_out = []
    for h in range(head_local):
        lanes_h = slice(h * HEAD_DIM, (h + 1) * HEAD_DIM)
        q = query[:, :, lanes_h]
        own_k = self_kv[:, :, 0, lanes_h]
        own_v = self_kv[:, :, 1, lanes_h]
        slope = slopes[h]
        own_scores = (
            jnp.einsum("mtd,msd->mts", q, own_k, preferred_element_type=jnp.float32) * score_scale
        )
        own_scores = own_scores - slope * own_distance[None]
        own_scores = jnp.where(own_allowed, own_scores, NEGATIVE)
        scores = (
            jnp.einsum("mtd,smjd->mtsj", q, page_keys[..., lanes_h],
                       preferred_element_type=jnp.float32).reshape(2, tok_grp, -1) * score_scale
        )
        scores = scores - slope * distance[None]
        scores = jnp.where(allowed, scores, NEGATIVE)
        row_top = jnp.maximum(jnp.max(scores, -1), jnp.max(own_scores, -1))
        exp_terms = jnp.where(allowed, jnp.exp(scores - row_top[..., None]), 0.0)
        own_terms = jnp.where(own_allowed, jnp.exp(own_scores - row_top[..., None]), 0.0)
        denominator = jnp.sum(exp_terms, -1) + jnp.sum(own_terms, -1)
        numerator = jnp.einsum(
            "mtsj,smjd->mtd",
            exp_terms.astype(jnp.bfloat16).reshape(2, tok_grp, buffer, page_len),
            page_values[..., lanes_h],
            preferred_element_type=jnp.float32,
        ) + jnp.einsum(
            "mts,msd->mtd", own_terms.astype(jnp.bfloat16), own_v,
            preferred_element_type=jnp.float32,
        )
        heads_out.append(numerator / denominator[..., None])
    attended = jnp.concatenate(heads_out, axis=-1).astype(jnp.bfloat16)

    rows_local = tok_grp // shards
    side = tensor_id % 2
    x_size = shards // 2
    x_id = tensor_id // 2
    swap = [(t, t ^ 1) for t in range(shards)]

    def x_shift(step):
        return [(t, (t + 2 * step) % shards) for t in range(shards)]

    partial = jnp.einsum("mtk,mkd->tmd", attended, out_proj, preferred_element_type=jnp.float32)
    partial = partial.reshape(x_size, 2, rows_local, 2, width)
    own_rows = jnp.transpose(residual.astype(jnp.float32), (1, 0, 2))
    partial = lax.dynamic_update_slice(
        partial,
        (lax.dynamic_slice(partial, (x_id, side, 0, 0, 0), (1, 1, rows_local, 2, width))
         + own_rows[None, None]),
        (x_id, side, 0, 0, 0),
    )
    pair_sum = lax.dynamic_index_in_dim(partial, side, 1, keepdims=False) + lax.ppermute(
        lax.dynamic_index_in_dim(partial, 1 - side, 1, keepdims=False), "tensor", swap
    )
    hidden = pair_sum
    for k in range(1, x_size):
        hidden = hidden + lax.ppermute(pair_sum, "tensor", x_shift(k))
    hidden = jnp.transpose(hidden.reshape(x_size * rows_local, 2, width), (1, 0, 2))
    row_mean = jnp.mean(hidden, axis=-1, keepdims=True)
    centered = hidden - row_mean
    variance = jnp.mean(centered * centered, axis=-1, keepdims=True)
    normed = (
        centered / jnp.sqrt(variance + EPSILON) * norm_gain[:, None, :] + norm_bias[:, None, :]
    ).astype(jnp.bfloat16)

    voc_local = vocab.shape[2]
    offset = (group_id * shards + tensor_id) * voc_local
    y_size = 4
    z_size = groups // y_size
    z_id = group_id // y_size
    y_id = group_id % y_size
    kept = lax.dynamic_index_in_dim(normed, side, 0, keepdims=False).reshape(x_size, rows_local, width)
    given = lax.ppermute(
        lax.dynamic_index_in_dim(normed, 1 - side, 0, keepdims=False), "tensor", swap
    ).reshape(x_size, rows_local, width)
    block = jnp.where(
        side == 0, jnp.stack([kept, given], 1), jnp.stack([given, kept], 1)
    ).reshape(tok_grp, width)

    def y_shift(step):
        return [(z * y_size + y, z * y_size + (y + step) % y_size)
                for z in range(z_size) for y in range(y_size)]

    def z_shift(step):
        return [(z * y_size + y, ((z + step) % z_size) * y_size + y)
                for z in range(z_size) for y in range(y_size)]

    block = jnp.concatenate(
        [block] + [lax.ppermute(block, "group", y_shift(k)) for k in range(1, y_size)], 0
    )
    forward, backward = block, block
    chunks = [block]
    z_from = [0]
    for k in range(1, z_size // 2):
        forward = lax.ppermute(forward, "group", z_shift(1))
        chunks.append(forward)
        z_from.append(k)
        backward = lax.ppermute(backward, "group", z_shift(z_size - 1))
        chunks.append(backward)
        z_from.append(z_size - k)
    split = block.shape[0] // 2
    chunks.append(jnp.concatenate([
        lax.ppermute(forward[:split], "group", z_shift(1)),
        lax.ppermute(backward[split:], "group", z_shift(z_size - 1)),
    ], 0))
    z_from.append(z_size // 2)
    own_model = jnp.concatenate(chunks, 0)
    other_model = lax.ppermute(own_model, "tensor", swap)
    z_from = jnp.array(z_from, dtype=jnp.int32)
    y_from = jnp.arange(y_size, dtype=jnp.int32)
    source_group = (
        ((z_id - z_from[:, None]) % z_size) * y_size + (y_id - y_from[None, :]) % y_size
    ).reshape(-1)
    wanted = (targets.reshape(groups, tok_grp)[source_group] - offset).reshape(-1)
    lanes = jnp.arange(voc_local, dtype=jnp.int32)

    def local_stats(rows, weights):
        logits = jnp.dot(rows, weights, preferred_element_type=jnp.float32)
        peak = jnp.max(logits, axis=1)
        total = jnp.sum(jnp.exp(logits - peak[:, None]), axis=1)
        chosen = jnp.sum(jnp.where(lanes[None, :] == wanted[:, None], logits, 0.0), axis=1)
        return jnp.stack([peak, total, chosen])

    own_stats = local_stats(own_model, lax.dynamic_index_in_dim(vocab, side, 0, keepdims=False))
    other_stats = local_stats(
        other_model, lax.dynamic_index_in_dim(vocab, 1 - side, 0, keepdims=False)
    )
    stats = jnp.where(
        side == 0, jnp.stack([own_stats, other_stats], 1), jnp.stack([other_stats, own_stats], 1)
    ).reshape(3, 2, groups, tok_grp)
    group_at = jnp.zeros((groups,), jnp.int32).at[source_group].set(
        jnp.arange(groups, dtype=jnp.int32)
    )
    stats = jnp.take(stats, group_at, axis=2)
    stats = stats.reshape(3, 2, groups, shards, rows_local)

    stats = lax.all_to_all(stats, "tensor", 3, 3, tiled=True)
    peak, total, chosen = lse_combine(stats[0], stats[1], stats[2], 2)
    stats = lax.all_to_all(jnp.stack([peak, total, chosen]), "group", 2, 2, tiled=True)
    peak, total, chosen = lse_combine(stats[0], stats[1], stats[2], 1)
    mine_lp = chosen - (peak + jnp.log(total))

    local_ids = tensor_id * rows_local + jnp.arange(rows_local, dtype=jnp.int32)
    keep_token = local_ids % SCORE_LEN < score_len[local_ids // SCORE_LEN]
    return jnp.where(keep_token[None, :], mine_lp, 0.0)


def solution(mesh):
    in_specs = (
        P(None, "group", "tensor"),
        P(None, "group", None, "tensor"),
        P(None, "group", None, None, "tensor"),
        P(),
        P(),
        P("group"),
        P(None, "tensor", None),
        P(None, ("group", "tensor"), None),
        P(),
        P(),
        P(None, None, ("group", "tensor")),
        P(),
    )
    out_specs = P(None, ("group", "tensor"))
    return jax.shard_map(
        per_device, mesh=mesh, in_specs=in_specs, out_specs=out_specs, check_vma=False
    )
```

```python
import math

import jax
import jax.numpy as jnp
from jax import lax
from jax.sharding import PartitionSpec as P

HEADS = 16
HEAD_DIM = 128
REQ_GRP = 2
SCORE_LEN = 16


NEGATIVE = -1e30
EPSILON = 1e-05


def alibi_slopes(head_count):
    return jnp.exp2(-8.0 * jnp.arange(1, head_count + 1).astype(jnp.float32) / head_count)


def lse_combine(peak, total, chosen, axis):
    top = jnp.max(peak, axis=axis, keepdims=True)
    total = jnp.sum(total * jnp.exp(peak - top), axis=axis)
    return jnp.squeeze(top, axis), total, jnp.sum(chosen, axis=axis)


def per_device(
    query,
    self_kv,
    kv_pages,
    page_dest,
    page_request,
    score_len,
    out_proj,
    residual,
    norm_gain,
    norm_bias,
    vocab,
    targets,
):
    groups = lax.axis_size("group")
    shards = lax.axis_size("tensor")
    group_id = lax.axis_index("group")
    tensor_id = lax.axis_index("tensor")
    tok_grp = query.shape[1]
    flat_width = query.shape[2]
    head_local = flat_width // HEAD_DIM
    per_owner = kv_pages.shape[1]
    page_len = kv_pages.shape[2]
    capacity = 2 * per_owner // groups
    destination = page_dest[:, 0]
    page_total = destination.shape[0]
    buffer = groups * capacity
    width = residual.shape[2]

    local = jnp.arange(per_owner, dtype=jnp.int32)
    earlier = local[None, :] < local[:, None]
    my_dest = lax.dynamic_slice_in_dim(destination, group_id * per_owner, per_owner)
    my_position = jnp.sum(
        ((my_dest[None, :] == my_dest[:, None]) & earlier).astype(jnp.int32), axis=1
    )
    out_slot = my_dest * capacity + my_position
    slots = jnp.arange(buffer, dtype=jnp.int32)
    send_hot = (out_slot[None, :] == slots[:, None]).astype(kv_pages.dtype)
    outgoing = jnp.einsum(
        "sp,mpjcx->scmjx", send_hot, kv_pages, preferred_element_type=jnp.float32
    ).astype(kv_pages.dtype)
    incoming = lax.all_to_all(
        outgoing.reshape(buffer, -1, flat_width), "group", split_axis=0, concat_axis=0, tiled=True
    ).reshape(outgoing.shape)

    pages = jnp.arange(page_total, dtype=jnp.int32)
    mine = destination == group_id
    mine_blocks = mine.reshape(groups, per_owner)
    rank_in_block = jnp.sum(
        (mine_blocks[:, None, :] & earlier[None]).astype(jnp.int32), axis=2
    ).reshape(-1)
    arrival = (pages // per_owner) * capacity + rank_in_block
    recv_hot = mine[None, :] & (arrival[None, :] == slots[:, None])
    is_valid = jnp.any(recv_hot, axis=1)
    slot_page = jnp.sum(jnp.where(recv_hot, pages[None, :], 0), axis=1)
    slot_request = jnp.sum(jnp.where(recv_hot, page_request[None, :], 0), axis=1)
    slot_rank = jnp.sum(
        (
            mine[None, :]
            & (page_request[None, :] == slot_request[:, None])
            & (pages[None, :] < slot_page[:, None])
        ).astype(jnp.int32),
        axis=1,
    )
    request_ids = jnp.arange(REQ_GRP, dtype=jnp.int32)
    totals = jnp.sum(
        (mine[None, :] & (page_request[None, :] == request_ids[:, None])).astype(jnp.int32),
        axis=1,
    )

    slopes = lax.dynamic_slice_in_dim(alibi_slopes(HEADS), tensor_id * head_local, head_local)
    score_scale = 1.0 / math.sqrt(HEAD_DIM)
    token_ids = jnp.arange(tok_grp, dtype=jnp.int32)
    token_request = token_ids // SCORE_LEN
    token_step = token_ids % SCORE_LEN
    own_distance = (token_step[:, None] - token_step[None, :]).astype(jnp.float32)
    own_allowed = (
        (token_request[:, None] == token_request[None, :])
        & (token_step[None, :] <= token_step[:, None])
    )[None]
    key_request = jnp.repeat(jnp.where(is_valid, slot_request, -1), page_len)
    key_position = (
        slot_rank[:, None] * page_len + jnp.arange(page_len, dtype=jnp.int32)[None, :]
    ).reshape(-1)
    context = totals[token_request] * page_len
    distance = ((context + token_step)[:, None] - key_position[None, :]).astype(jnp.float32)
    allowed = (key_request[None, :] == token_request[:, None])[None]
    page_keys = incoming[:, 0]
    page_values = incoming[:, 1]
    heads_out = []
    for h in range(head_local):
        lanes_h = slice(h * HEAD_DIM, (h + 1) * HEAD_DIM)
        q = query[:, :, lanes_h]
        own_k = self_kv[:, :, 0, lanes_h]
        own_v = self_kv[:, :, 1, lanes_h]
        slope = slopes[h]
        own_scores = (
            jnp.einsum("mtd,msd->mts", q, own_k, preferred_element_type=jnp.float32) * score_scale
        )
        own_scores = own_scores - slope * own_distance[None]
        own_scores = jnp.where(own_allowed, own_scores, NEGATIVE)
        scores = (
            jnp.einsum("mtd,smjd->mtsj", q, page_keys[..., lanes_h],
                       preferred_element_type=jnp.float32).reshape(2, tok_grp, -1) * score_scale
        )
        scores = scores - slope * distance[None]
        scores = jnp.where(allowed, scores, NEGATIVE)
        row_top = jnp.maximum(jnp.max(scores, -1), jnp.max(own_scores, -1))
        exp_terms = jnp.where(allowed, jnp.exp(scores - row_top[..., None]), 0.0)
        own_terms = jnp.where(own_allowed, jnp.exp(own_scores - row_top[..., None]), 0.0)
        denominator = jnp.sum(exp_terms, -1) + jnp.sum(own_terms, -1)
        numerator = jnp.einsum(
            "mtsj,smjd->mtd",
            exp_terms.astype(jnp.bfloat16).reshape(2, tok_grp, buffer, page_len),
            page_values[..., lanes_h],
            preferred_element_type=jnp.float32,
        ) + jnp.einsum(
            "mts,msd->mtd", own_terms.astype(jnp.bfloat16), own_v,
            preferred_element_type=jnp.float32,
        )
        heads_out.append(numerator / denominator[..., None])
    attended = jnp.concatenate(heads_out, axis=-1).astype(jnp.bfloat16)

    rows_local = tok_grp // shards
    side = tensor_id % 2
    x_size = shards // 2
    x_id = tensor_id // 2
    swap = [(t, t ^ 1) for t in range(shards)]

    partial = jnp.einsum("mtk,mkd->tmd", attended, out_proj, preferred_element_type=jnp.float32)
    partial = partial.reshape(x_size, 2, rows_local, 2, width)
    own_rows = jnp.transpose(residual.astype(jnp.float32), (1, 0, 2))
    partial = lax.dynamic_update_slice(
        partial,
        (lax.dynamic_slice(partial, (x_id, side, 0, 0, 0), (1, 1, rows_local, 2, width))
         + own_rows[None, None]),
        (x_id, side, 0, 0, 0),
    )
    pair_sum = lax.dynamic_index_in_dim(partial, side, 1, keepdims=False) + lax.ppermute(
        lax.dynamic_index_in_dim(partial, 1 - side, 1, keepdims=False), "tensor", swap
    )
    hidden = pair_sum
    step = 2
    while step < shards:
        hidden = hidden + lax.ppermute(hidden, "tensor", [(t, t ^ step) for t in range(shards)])
        step *= 2
    hidden = jnp.transpose(hidden.reshape(x_size * rows_local, 2, width), (1, 0, 2))
    row_mean = jnp.mean(hidden, axis=-1, keepdims=True)
    centered = hidden - row_mean
    variance = jnp.mean(centered * centered, axis=-1, keepdims=True)
    normed = (
        centered / jnp.sqrt(variance + EPSILON) * norm_gain[:, None, :] + norm_bias[:, None, :]
    ).astype(jnp.bfloat16)

    voc_local = vocab.shape[2]
    offset = (group_id * shards + tensor_id) * voc_local
    y_size = 4
    z_size = groups // y_size
    z_id = group_id // y_size
    y_id = group_id % y_size
    kept = lax.dynamic_index_in_dim(normed, side, 0, keepdims=False).reshape(x_size, rows_local, width)
    given = lax.ppermute(
        lax.dynamic_index_in_dim(normed, 1 - side, 0, keepdims=False), "tensor", swap
    ).reshape(x_size, rows_local, width)
    block = jnp.where(
        side == 0, jnp.stack([kept, given], 1), jnp.stack([given, kept], 1)
    ).reshape(tok_grp, width)

    def y_shift(step):
        return [(z * y_size + y, z * y_size + (y + step) % y_size)
                for z in range(z_size) for y in range(y_size)]

    def z_shift(step):
        return [(z * y_size + y, ((z + step) % z_size) * y_size + y)
                for z in range(z_size) for y in range(y_size)]

    block = jnp.concatenate(
        [block] + [lax.ppermute(block, "group", y_shift(k)) for k in range(1, y_size)], 0
    )
    forward, backward = block, block
    chunks = [block]
    z_from = [0]
    for k in range(1, z_size // 2):
        forward = lax.ppermute(forward, "group", z_shift(1))
        chunks.append(forward)
        z_from.append(k)
        backward = lax.ppermute(backward, "group", z_shift(z_size - 1))
        chunks.append(backward)
        z_from.append(z_size - k)
    split = block.shape[0] // 2
    chunks.append(jnp.concatenate([
        lax.ppermute(forward[:split], "group", z_shift(1)),
        lax.ppermute(backward[split:], "group", z_shift(z_size - 1)),
    ], 0))
    z_from.append(z_size // 2)
    own_model = jnp.concatenate(chunks, 0)
    other_model = lax.ppermute(own_model, "tensor", swap)
    z_from = jnp.array(z_from, dtype=jnp.int32)
    y_from = jnp.arange(y_size, dtype=jnp.int32)
    source_group = (
        ((z_id - z_from[:, None]) % z_size) * y_size + (y_id - y_from[None, :]) % y_size
    ).reshape(-1)
    wanted = (targets.reshape(groups, tok_grp)[source_group] - offset).reshape(-1)
    lanes = jnp.arange(voc_local, dtype=jnp.int32)

    def local_stats(rows, weights):
        logits = jnp.dot(rows, weights, preferred_element_type=jnp.float32)
        peak = jnp.max(logits, axis=1)
        total = jnp.sum(jnp.exp(logits - peak[:, None]), axis=1)
        chosen = jnp.sum(jnp.where(lanes[None, :] == wanted[:, None], logits, 0.0), axis=1)
        return jnp.stack([peak, total, chosen])

    own_stats = local_stats(own_model, lax.dynamic_index_in_dim(vocab, side, 0, keepdims=False))
    other_stats = local_stats(
        other_model, lax.dynamic_index_in_dim(vocab, 1 - side, 0, keepdims=False)
    )
    stats = jnp.where(
        side == 0, jnp.stack([own_stats, other_stats], 1), jnp.stack([other_stats, own_stats], 1)
    ).reshape(3, 2, groups, tok_grp)
    group_at = jnp.zeros((groups,), jnp.int32).at[source_group].set(
        jnp.arange(groups, dtype=jnp.int32)
    )
    stats = jnp.take(stats, group_at, axis=2)
    stats = stats.reshape(3, 2, groups, shards, rows_local)

    stats = lax.all_to_all(stats, "tensor", 3, 3, tiled=True)
    peak, total, chosen = lse_combine(stats[0], stats[1], stats[2], 2)
    stats = lax.all_to_all(jnp.stack([peak, total, chosen]), "group", 2, 2, tiled=True)
    peak, total, chosen = lse_combine(stats[0], stats[1], stats[2], 1)
    mine_lp = chosen - (peak + jnp.log(total))

    local_ids = tensor_id * rows_local + jnp.arange(rows_local, dtype=jnp.int32)
    keep_token = local_ids % SCORE_LEN < score_len[local_ids // SCORE_LEN]
    return jnp.where(keep_token[None, :], mine_lp, 0.0)


def solution(mesh):
    in_specs = (
        P(None, "group", "tensor"),
        P(None, "group", None, "tensor"),
        P(None, "group", None, None, "tensor"),
        P(),
        P(),
        P("group"),
        P(None, "tensor", None),
        P(None, ("group", "tensor"), None),
        P(),
        P(),
        P(None, None, ("group", "tensor")),
        P(),
    )
    out_specs = P(None, ("group", "tensor"))
    return jax.shard_map(
        per_device, mesh=mesh, in_specs=in_specs, out_specs=out_specs, check_vma=False
    )
```

```python
import math

import jax
import jax.numpy as jnp
from jax import lax
from jax.sharding import PartitionSpec as P

HEADS = 16
HEAD_DIM = 128
REQ_GRP = 2
SCORE_LEN = 16


NEGATIVE = -1e30
EPSILON = 1e-05


def alibi_slopes(head_count):
    return jnp.exp2(-8.0 * jnp.arange(1, head_count + 1).astype(jnp.float32) / head_count)


def lse_combine(peak, total, chosen, axis):
    top = jnp.max(peak, axis=axis, keepdims=True)
    total = jnp.sum(total * jnp.exp(peak - top), axis=axis)
    return jnp.squeeze(top, axis), total, jnp.sum(chosen, axis=axis)


def per_device(
    query,
    self_kv,
    kv_pages,
    page_dest,
    page_request,
    score_len,
    out_proj,
    residual,
    norm_gain,
    norm_bias,
    vocab,
    targets,
):
    groups = lax.axis_size("group")
    shards = lax.axis_size("tensor")
    group_id = lax.axis_index("group")
    tensor_id = lax.axis_index("tensor")
    tok_grp = query.shape[1]
    flat_width = query.shape[2]
    head_local = flat_width // HEAD_DIM
    per_owner = kv_pages.shape[1]
    page_len = kv_pages.shape[2]
    capacity = 2 * per_owner // groups
    destination = page_dest[:, 0]
    page_total = destination.shape[0]
    buffer = groups * capacity
    width = residual.shape[2]

    local = jnp.arange(per_owner, dtype=jnp.int32)
    earlier = local[None, :] < local[:, None]
    my_dest = lax.dynamic_slice_in_dim(destination, group_id * per_owner, per_owner)
    my_position = jnp.sum(
        ((my_dest[None, :] == my_dest[:, None]) & earlier).astype(jnp.int32), axis=1
    )
    out_slot = my_dest * capacity + my_position
    slots = jnp.arange(buffer, dtype=jnp.int32)
    send_hot = (out_slot[None, :] == slots[:, None]).astype(kv_pages.dtype)
    outgoing = jnp.einsum(
        "sp,mpjcx->scmjx", send_hot, kv_pages, preferred_element_type=jnp.float32
    ).astype(kv_pages.dtype)
    incoming = [
        lax.all_to_all(
            outgoing[:, :, m].reshape(buffer, -1, flat_width), "group", 0, 0, tiled=True
        ).reshape(buffer, 2, 1, page_len, flat_width)
        for m in range(2)
    ]

    pages = jnp.arange(page_total, dtype=jnp.int32)
    mine = destination == group_id
    mine_blocks = mine.reshape(groups, per_owner)
    rank_in_block = jnp.sum(
        (mine_blocks[:, None, :] & earlier[None]).astype(jnp.int32), axis=2
    ).reshape(-1)
    arrival = (pages // per_owner) * capacity + rank_in_block
    recv_hot = mine[None, :] & (arrival[None, :] == slots[:, None])
    is_valid = jnp.any(recv_hot, axis=1)
    slot_page = jnp.sum(jnp.where(recv_hot, pages[None, :], 0), axis=1)
    slot_request = jnp.sum(jnp.where(recv_hot, page_request[None, :], 0), axis=1)
    slot_rank = jnp.sum(
        (
            mine[None, :]
            & (page_request[None, :] == slot_request[:, None])
            & (pages[None, :] < slot_page[:, None])
        ).astype(jnp.int32),
        axis=1,
    )
    request_ids = jnp.arange(REQ_GRP, dtype=jnp.int32)
    totals = jnp.sum(
        (mine[None, :] & (page_request[None, :] == request_ids[:, None])).astype(jnp.int32),
        axis=1,
    )

    slopes = lax.dynamic_slice_in_dim(alibi_slopes(HEADS), tensor_id * head_local, head_local)
    score_scale = 1.0 / math.sqrt(HEAD_DIM)
    token_ids = jnp.arange(tok_grp, dtype=jnp.int32)
    token_request = token_ids // SCORE_LEN
    token_step = token_ids % SCORE_LEN
    own_distance = (token_step[:, None] - token_step[None, :]).astype(jnp.float32)
    own_allowed = (
        (token_request[:, None] == token_request[None, :])
        & (token_step[None, :] <= token_step[:, None])
    )[None]
    key_request = jnp.repeat(jnp.where(is_valid, slot_request, -1), page_len)
    key_position = (
        slot_rank[:, None] * page_len + jnp.arange(page_len, dtype=jnp.int32)[None, :]
    ).reshape(-1)
    context = totals[token_request] * page_len
    distance = ((context + token_step)[:, None] - key_position[None, :]).astype(jnp.float32)
    allowed = (key_request[None, :] == token_request[:, None])[None]
    model_out = []
    for m in range(2):
        page_keys = incoming[m][:, 0]
        page_values = incoming[m][:, 1]
        heads_out = []
        for h in range(head_local):
            lanes_h = slice(h * HEAD_DIM, (h + 1) * HEAD_DIM)
            q = query[m:m + 1, :, lanes_h]
            own_k = self_kv[m:m + 1, :, 0, lanes_h]
            own_v = self_kv[m:m + 1, :, 1, lanes_h]
            slope = slopes[h]
            own_scores = (
                jnp.einsum("mtd,msd->mts", q, own_k, preferred_element_type=jnp.float32) * score_scale
            )
            own_scores = own_scores - slope * own_distance[None]
            own_scores = jnp.where(own_allowed, own_scores, NEGATIVE)
            scores = (
                jnp.einsum("mtd,smjd->mtsj", q, page_keys[..., lanes_h],
                           preferred_element_type=jnp.float32).reshape(1, tok_grp, -1) * score_scale
            )
            scores = scores - slope * distance[None]
            scores = jnp.where(allowed, scores, NEGATIVE)
            row_top = jnp.maximum(jnp.max(scores, -1), jnp.max(own_scores, -1))
            exp_terms = jnp.where(allowed, jnp.exp(scores - row_top[..., None]), 0.0)
            own_terms = jnp.where(own_allowed, jnp.exp(own_scores - row_top[..., None]), 0.0)
            denominator = jnp.sum(exp_terms, -1) + jnp.sum(own_terms, -1)
            numerator = jnp.einsum(
                "mtsj,smjd->mtd",
                exp_terms.astype(jnp.bfloat16).reshape(1, tok_grp, buffer, page_len),
                page_values[..., lanes_h],
                preferred_element_type=jnp.float32,
            ) + jnp.einsum(
                "mts,msd->mtd", own_terms.astype(jnp.bfloat16), own_v,
                preferred_element_type=jnp.float32,
            )
            heads_out.append(numerator / denominator[..., None])
        model_out.append(jnp.concatenate(heads_out, axis=-1))
    attended = jnp.concatenate(model_out, axis=0).astype(jnp.bfloat16)

    rows_local = tok_grp // shards
    partial = jnp.einsum("mtk,mkd->tmd", attended, out_proj, preferred_element_type=jnp.float32)
    parts = lax.all_to_all(
        partial.reshape(shards, rows_local, 2, width), "tensor", 0, 0, tiled=True
    )
    mixed = jnp.sum(parts, axis=0)
    hidden = residual.astype(jnp.float32) + jnp.transpose(mixed, (1, 0, 2))
    row_mean = jnp.mean(hidden, axis=-1, keepdims=True)
    centered = hidden - row_mean
    variance = jnp.mean(centered * centered, axis=-1, keepdims=True)
    normed = (
        centered / jnp.sqrt(variance + EPSILON) * norm_gain[:, None, :] + norm_bias[:, None, :]
    ).astype(jnp.bfloat16)

    voc_local = vocab.shape[2]
    offset = (group_id * shards + tensor_id) * voc_local
    side = tensor_id % 2
    x_size = shards // 2
    x_id = tensor_id // 2
    y_size = 4
    z_size = groups // y_size
    z_id = group_id // y_size
    y_id = group_id % y_size
    swap = [(t, t ^ 1) for t in range(shards)]
    kept = lax.dynamic_index_in_dim(normed, side, 0, keepdims=False)
    given = lax.ppermute(lax.dynamic_index_in_dim(normed, 1 - side, 0, keepdims=False), "tensor", swap)
    block = jnp.where(
        side == 0, jnp.concatenate([kept, given], 0), jnp.concatenate([given, kept], 0)
    )

    def x_shift(step):
        return [(t, (t + 2 * step) % shards) for t in range(shards)]

    def y_shift(step):
        return [(z * y_size + y, z * y_size + (y + step) % y_size)
                for z in range(z_size) for y in range(y_size)]

    def z_shift(step):
        return [(z * y_size + y, ((z + step) % z_size) * y_size + y)
                for z in range(z_size) for y in range(y_size)]

    block = jnp.concatenate(
        [block] + [lax.ppermute(block, "tensor", x_shift(k)) for k in range(1, x_size)], 0
    )
    block = jnp.concatenate(
        [block] + [lax.ppermute(block, "group", y_shift(k)) for k in range(1, y_size)], 0
    )
    forward, backward = block, block
    chunks = [block]
    z_from = [0]
    for k in range(1, z_size // 2):
        forward = lax.ppermute(forward, "group", z_shift(1))
        chunks.append(forward)
        z_from.append(k)
        backward = lax.ppermute(backward, "group", z_shift(z_size - 1))
        chunks.append(backward)
        z_from.append(z_size - k)
    split = block.shape[0] // 2
    chunks.append(jnp.concatenate([
        lax.ppermute(forward[:split], "group", z_shift(1)),
        lax.ppermute(backward[split:], "group", z_shift(z_size - 1)),
    ], 0))
    z_from.append(z_size // 2)
    own_model = jnp.concatenate(chunks, 0)
    other_model = lax.ppermute(own_model, "tensor", swap)
    z_from = jnp.array(z_from, dtype=jnp.int32)
    y_from = jnp.arange(y_size, dtype=jnp.int32)
    source_group = (
        ((z_id - z_from[:, None]) % z_size) * y_size + (y_id - y_from[None, :]) % y_size
    ).reshape(-1)
    x_from = (x_id - jnp.arange(x_size, dtype=jnp.int32)) % x_size
    pair_rows = 2 * rows_local
    wanted = (
        targets.reshape(groups, x_size, pair_rows)[source_group[:, None], x_from[None, :]] - offset
    ).reshape(-1)
    lanes = jnp.arange(voc_local, dtype=jnp.int32)

    def local_stats(rows, weights):
        logits = jnp.dot(rows, weights, preferred_element_type=jnp.float32)
        peak = jnp.max(logits, axis=1)
        total = jnp.sum(jnp.exp(logits - peak[:, None]), axis=1)
        chosen = jnp.sum(jnp.where(lanes[None, :] == wanted[:, None], logits, 0.0), axis=1)
        return jnp.stack([peak, total, chosen])

    own_stats = local_stats(own_model, lax.dynamic_index_in_dim(vocab, side, 0, keepdims=False))
    other_stats = local_stats(
        other_model, lax.dynamic_index_in_dim(vocab, 1 - side, 0, keepdims=False)
    )
    stats = jnp.where(
        side == 0, jnp.stack([own_stats, other_stats], 1), jnp.stack([other_stats, own_stats], 1)
    ).reshape(3, 2, groups, x_size, pair_rows)
    group_at = jnp.zeros((groups,), jnp.int32).at[source_group].set(
        jnp.arange(groups, dtype=jnp.int32)
    )
    x_at = (x_id - jnp.arange(x_size, dtype=jnp.int32)) % x_size
    stats = jnp.take(jnp.take(stats, group_at, axis=2), x_at, axis=3)
    stats = stats.reshape(3, 2, groups, shards, rows_local)

    stats = lax.all_to_all(stats, "tensor", 3, 3, tiled=True)
    peak, total, chosen = lse_combine(stats[0], stats[1], stats[2], 2)
    stats = lax.all_to_all(jnp.stack([peak, total, chosen]), "group", 2, 2, tiled=True)
    peak, total, chosen = lse_combine(stats[0], stats[1], stats[2], 1)
    mine_lp = chosen - (peak + jnp.log(total))

    local_ids = tensor_id * rows_local + jnp.arange(rows_local, dtype=jnp.int32)
    keep_token = local_ids % SCORE_LEN < score_len[local_ids // SCORE_LEN]
    return jnp.where(keep_token[None, :], mine_lp, 0.0)


def solution(mesh):
    in_specs = (
        P(None, "group", "tensor"),
        P(None, "group", None, "tensor"),
        P(None, "group", None, None, "tensor"),
        P(),
        P(),
        P("group"),
        P(None, "tensor", None),
        P(None, ("group", "tensor"), None),
        P(),
        P(),
        P(None, None, ("group", "tensor")),
        P(),
    )
    out_specs = P(None, ("group", "tensor"))
    return jax.shard_map(
        per_device, mesh=mesh, in_specs=in_specs, out_specs=out_specs, check_vma=False
    )
```
